128 devices in a mesh: tm: 4 (over x), space: 16 (over z, y), ens: 2 (over core).
Axes of the slice: x: 4, y: 4, z: 4, core: 2. Of those that a mesh axis runs over, the one named last changes fastest.
Arguments:
- start_states: float32 [4, 16, 1024, 1024], P('tm', 'ens', 'space'), may hold values from -6 to 6
- velocity_x: float32 [1024, 1024], P('space'), may hold values from -0.15 to 0.15
- velocity_y: float32 [1024, 1024], P('space'), may hold values from -0.15 to 0.15
- diffusivity: float32 [1024, 1024], P('space'), may hold values from 0.06 to 0.2
- source_shape: float32 [1024, 1024], P('space'), may hold values from -6 to 6
- params: float32 [16, 128], P('ens'), may hold values from -6 to 6
- obs_cell: int32 [4, 1024], P('tm', 'space'), may hold values from 0 to 1048575, as said below
- obs_data: float32 [4, 1024], P('tm', 'space'), may hold values from -6 to 6
- obs_noise: float32 [4, 1024, 16], P('tm', 'space'), may hold values from -6 to 6
- obs_var: float32 [4, 1024], P('tm', 'space'), may hold values from 0.05 to 0.5
Outputs:
- new_states: float32 [4, 16, 1024, 1024], P('tm', 'ens', 'space')
- new_params: float32 [16, 128], P('ens')
The draws below stay inside these ranges and needn't reach their ends.
Inputs may be any that keep to these rules, and one draw needn't show every extreme that they name: `obs_cell`: entry (n, o) lies in the rows of slab o // 64, that is row (o // 64) * 64 up to 63 rows further.
All inputs are finite; a program needn't handle non-finite values.
Results may differ from the reference program's by a relative error of at most 0.0003.
Values sent between devices are 32-bit elements; how exact they have to be, the bound alone decides.
No kernel may reach another device: no remote copies, remote signals or barrier semaphores. Data moves between devices by JAX's collectives and lax.ppermute only.
A program may use at most 128 MiB of HBM per device.

```python
import math
import jax
import jax.numpy as jnp
from jax import lax

ROWS_DEV = 64
COLS = 1024
FINE = 4
PARAMS = 128
OBS_DEV = 64
SLICES = 4
MEMBERS = 16
NY = 1024
OBS = 1024
BAND = 8


def draw_obs_cell(key, part):
    offsets = jax.random.randint(key, (SLICES, OBS), 0, ROWS_DEV * COLS)
    slab_of = jnp.arange(OBS, dtype=jnp.int32) // OBS_DEV * (ROWS_DEV * COLS)
    cells = offsets.astype(jnp.int32) + slab_of[None, :]
    cells = cells.at[0, 0].set(0)
    cells = cells.at[SLICES - 1, OBS - 1].set(NY * COLS - 1)
    return cells.astype(jnp.int32)


def levels(rng, dims, pieces, low, top_value):
    def one(dim, shards_of):
        heights = jax.random.uniform(jax.random.fold_in(jax.random.fold_in(rng, 6), dim), (shards_of,), jnp.float32, low / len(pieces), top_value / len(pieces))
        return jnp.repeat(jnp.exp(heights), dims[dim] // shards_of).reshape((-1,) + (1,) * (len(dims) - dim - 1))

    loudness = one(*pieces[0])
    for cut in pieces[1:]:
        loudness = loudness * one(*cut)
    return loudness


def centred(key, shape, scale, most, pieces=(), held_as=jnp.bfloat16):
    gain = levels(key, shape, pieces, -0.22, 0.18) if pieces else 1.0
    drawn = jax.random.normal(key, shape, jnp.float32) * scale * gain
    return jnp.minimum(jnp.maximum(drawn, -most), most).astype(held_as)


def setup_inputs(seed: int = 0) -> dict:
    arg_keys = jax.random.split(jax.random.key(seed), 11)
    start_states = centred(arg_keys[0], (SLICES, MEMBERS, NY, COLS), 1.0, 6.0, ((0, 4), (1, 2), (2, 16)), jnp.float32)
    velocity_x = jnp.clip(jax.random.uniform(arg_keys[1], (NY, COLS), jnp.float32, -0.15, 0.15) * levels(arg_keys[1], (NY, COLS), ((0, 16),), -0.4, 0.0), -0.15, 0.15)
    velocity_y = jnp.clip(jax.random.uniform(arg_keys[2], (NY, COLS), jnp.float32, -0.15, 0.15) * levels(arg_keys[2], (NY, COLS), ((0, 16),), -0.4, 0.0), -0.15, 0.15)
    diffusivity = jnp.clip(jnp.exp(math.log(0.2) - 1.2039728 * jax.random.uniform(arg_keys[3], (NY, COLS), jnp.float32) ** levels(arg_keys[3], (NY, COLS), ((0, 16),), -0.2, 0.2)), 0.06, 0.2)
    source_shape = centred(arg_keys[4], (NY, COLS), 1.0, 6.0, ((0, 16),), jnp.float32)
    params = centred(arg_keys[5], (MEMBERS, PARAMS), 1.0, 6.0, ((0, 2),), jnp.float32)
    obs_cell = draw_obs_cell(jax.random.fold_in(arg_keys[10], 71), 0)
    obs_data = centred(arg_keys[7], (SLICES, OBS), 1.0, 6.0, ((0, 4), (1, 16)), jnp.float32)
    obs_noise = centred(arg_keys[8], (SLICES, OBS, MEMBERS), 0.5, 6.0, ((0, 4), (1, 16)), jnp.float32)
    obs_var = jnp.clip(jnp.exp(math.log(0.5) - 2.3025851 * jax.random.uniform(arg_keys[9], (SLICES, OBS), jnp.float32) ** levels(arg_keys[9], (SLICES, OBS), ((0, 4), (1, 16)), -0.2, 0.2)), 0.05, 0.5)
    return dict(start_states=start_states, velocity_x=velocity_x, velocity_y=velocity_y, diffusivity=diffusivity, source_shape=source_shape, params=params, obs_cell=obs_cell, obs_data=obs_data, obs_noise=obs_noise, obs_var=obs_var)


FINE_DT = 0.25

def advance(values_in, coeffs, inside, step_size, forcing):
    middle = values_in[:, 1:-1, :]
    above_row = values_in[:, :-2, :]
    below_row = values_in[:, 2:, :]
    west_cell = jnp.pad(middle[:, :, :-1], ((0, 0), (0, 0), (1, 0)))
    east_cell = jnp.pad(middle[:, :, 1:], ((0, 0), (0, 0), (0, 1)))
    spread_term = coeffs[0] * (above_row + below_row + west_cell + east_cell - 4.0 * middle)
    tendency = spread_term - coeffs[1] * (east_cell - west_cell) * 0.5 - coeffs[2] * (below_row - above_row) * 0.5
    if forcing is not None:
        tendency = tendency + forcing
    return (middle + step_size * tendency) * inside

def padded(values_in):
    return jnp.pad(values_in, ((0, 0), (1, 1), (0, 0)))

def reference(start_states, velocity_x, velocity_y, diffusivity, source_shape, params, obs_cell, obs_data, obs_noise, obs_var):
    coarse_dt = FINE_DT * FINE
    coeffs = jnp.stack([diffusivity, velocity_x, velocity_y])
    inside = jnp.ones((NY, 1), jnp.float32)
    forcing = source_shape[None] * jnp.repeat(params, BAND, axis=1)[:, None, :]
    results = []
    running = None
    for slice_no in range(SLICES):
        state = start_states[slice_no]
        current = state
        for section in range(FINE):
            current = advance(padded(current), coeffs, inside, FINE_DT, forcing)
        if slice_no == 0:
            running = current
        else:
            correction = current - advance(padded(state), coeffs, inside, coarse_dt, None)
            running = correction + advance(padded(running), coeffs, inside, coarse_dt, None)
        results.append(running)
    new_states = jnp.stack(results)
    flat = new_states.reshape(SLICES, MEMBERS, NY * COLS)
    where_obs = jnp.broadcast_to(obs_cell[:, None, :], (SLICES, MEMBERS, OBS))
    predicted = jnp.take_along_axis(flat, where_obs, axis=2)
    norm_factor = 1.0 / math.sqrt(MEMBERS - 1)
    inv_spread = lax.rsqrt(obs_var)[:, None, :]
    pred_mean = lax.optimization_barrier(jnp.mean(predicted, axis=1, keepdims=True))
    anomaly = (predicted - pred_mean) * (inv_spread * norm_factor)
    misfit = (obs_data[:, None, :] + jnp.transpose(obs_noise, (0, 2, 1)) - predicted) * inv_spread
    gram = jnp.einsum('sjo,sko->jk', anomaly, anomaly, precision=lax.Precision.HIGHEST)
    cross = jnp.einsum('sjo,sko->jk', anomaly, misfit, precision=lax.Precision.HIGHEST)
    system = jnp.eye(MEMBERS, dtype=jnp.float32) + gram
    factor = jnp.linalg.cholesky(system)
    weights = jax.scipy.linalg.cho_solve((factor, True), cross)
    param_anom = params - lax.optimization_barrier(jnp.mean(params, axis=0))
    new_params = params + jnp.dot(weights.T, param_anom, precision=lax.Precision.HIGHEST) * norm_factor
    return (new_states, new_params)
```

```python
import math

import jax
import jax.numpy as jnp
from jax import lax
from jax.sharding import PartitionSpec as P

FINE = 4


FINE_DT = 0.25


def with_halo(cells, axis, width):
    count = lax.axis_size(axis)
    ends = count - 1
    head = cells[:, :width]
    tail = cells[:, cells.shape[1] - width :]
    return jnp.concatenate(
        [
            lax.ppermute(tail, axis, [(i, i + 1) for i in range(ends)]),
            cells,
            lax.ppermute(head, axis, [(i + 1, i) for i in range(ends)]),
        ],
        axis=1,
    )


def butterfly_sum(value, axis):
    count = lax.axis_size(axis)
    if count & (count - 1):
        return lax.psum(value, axis)
    bit = 1
    while bit < count:
        value = value + lax.ppermute(value, axis, [(i, i ^ bit) for i in range(count)])
        bit *= 2
    return value


def both_halves(value, axis):
    other = lax.ppermute(value, axis, [(0, 1), (1, 0)])
    first = lax.axis_index(axis) == 0
    return jnp.where(first, jnp.concatenate([value, other]), jnp.concatenate([other, value]))


def advance(values_in, coeffs, inside, step_size, forcing):
    middle = values_in[:, 1:-1, :]
    above_row = values_in[:, :-2, :]
    below_row = values_in[:, 2:, :]
    west_cell = jnp.pad(middle[:, :, :-1], ((0, 0), (0, 0), (1, 0)))
    east_cell = jnp.pad(middle[:, :, 1:], ((0, 0), (0, 0), (0, 1)))
    spread_term = coeffs[0] * (above_row + below_row + west_cell + east_cell - 4.0 * middle)
    tendency = (
        spread_term
        - coeffs[1] * (east_cell - west_cell) * 0.5
        - coeffs[2] * (below_row - above_row) * 0.5
    )
    if forcing is not None:
        tendency = tendency + forcing
    return (middle + step_size * tendency) * inside


def per_device(
    start_states,
    velocity_x,
    velocity_y,
    diffusivity,
    source_shape,
    params,
    obs_cell,
    obs_data,
    obs_noise,
    obs_var,
):
    coarse_dt = FINE_DT * FINE
    state = start_states[0]
    members_here, row_count, col_count = state.shape
    slabs = row_count * lax.axis_size("space")
    first_row = lax.axis_index("space") * row_count
    slice_index = lax.axis_index("tm")
    links = lax.axis_size("tm") - 1
    depth = FINE + links
    band_width = col_count // params.shape[1]
    spread_params = jnp.repeat(params, band_width, axis=1)

    fields = jnp.stack([diffusivity, velocity_x, velocity_y, source_shape])
    wide = with_halo(jnp.concatenate([state, fields]), "space", depth)
    wide_state = wide[:members_here]
    wide_coeffs = wide[members_here : members_here + 3]
    wide_forcing = wide[members_here + 3][None] * spread_params[:, None, :]
    global_rows = first_row - depth + jnp.arange(row_count + 2 * depth, dtype=jnp.int32)
    wide_inside = ((global_rows >= 0) & (global_rows < slabs)).astype(jnp.float32)[:, None]

    def step(values, low, step_size, forcing):
        n = values.shape[1]
        lo, hi = low + 1, low + n - 1
        q = None if forcing is None else forcing[:, lo:hi]
        return advance(values, wide_coeffs[:, lo:hi], wide_inside[lo:hi], step_size, q)

    current = wide_state
    coarse_part = step(wide_state, 0, coarse_dt, None)
    for section in range(FINE):
        current = step(current, section, FINE_DT, wide_forcing)
    coarse_part = coarse_part[:, FINE - 1 : FINE - 1 + current.shape[1]]
    correction = jnp.where(slice_index > 0, current - coarse_part, current)
    running = correction
    for link in range(1, links + 1):
        earlier = lax.ppermute(running, "tm", [(i, i + 1) for i in range(links)])
        stepped = step(earlier, FINE + link - 1, coarse_dt, None)
        running = correction[:, link : correction.shape[1] - link] + stepped
    new_states = running[None]

    local_cell = obs_cell[0] - first_row * col_count
    rows = local_cell // col_count
    cols = local_cell % col_count
    predicted = running[:, rows, cols]
    every_pred = both_halves(predicted, "ens")
    every_param = both_halves(params, "ens")
    total = every_pred.shape[0]
    norm_factor = 1.0 / math.sqrt(total - 1)
    inv_spread = lax.rsqrt(obs_var[0])[None, :]
    pred_mean = jnp.mean(every_pred, axis=0, keepdims=True)
    anomaly = (every_pred - pred_mean) * (inv_spread * norm_factor)
    misfit = (obs_data[0][None, :] + obs_noise[0].T - every_pred) * inv_spread
    gram = jnp.dot(anomaly, anomaly.T, precision=lax.Precision.HIGHEST)
    cross = jnp.dot(anomaly, misfit.T, precision=lax.Precision.HIGHEST)
    sums = jnp.stack([gram, cross])
    sums = butterfly_sum(sums, "tm")
    sums = butterfly_sum(sums, "space")
    gram, cross = sums[0], sums[1]
    system = jnp.eye(total, dtype=jnp.float32) + gram
    factor = jnp.linalg.cholesky(system)
    weights = jax.scipy.linalg.cho_solve((factor, True), cross)
    param_anom = every_param - jnp.mean(every_param, axis=0)
    own_weights = lax.dynamic_slice_in_dim(
        weights, lax.axis_index("ens") * members_here, members_here, 1
    )
    new_params = (
        params + jnp.dot(own_weights.T, param_anom, precision=lax.Precision.HIGHEST) * norm_factor
    )
    return (new_states, new_params)


def solution(mesh):
    in_specs = (
        P("tm", "ens", "space", None),
        P("space", None),
        P("space", None),
        P("space", None),
        P("space", None),
        P("ens", None),
        P("tm", "space"),
        P("tm", "space"),
        P("tm", "space", None),
        P("tm", "space"),
    )
    out_specs = (P("tm", "ens", "space", None), P("ens", None))
    return jax.shard_map(
        per_device, mesh=mesh, in_specs=in_specs, out_specs=out_specs, check_vma=False
    )
```

```python
import math

import jax
import jax.numpy as jnp
from jax import lax
from jax.sharding import PartitionSpec as P

FINE = 4


FINE_DT = 0.25


def with_halo(cells, axis, width):
    count = lax.axis_size(axis)
    ends = count - 1
    head = cells[:, :width]
    tail = cells[:, cells.shape[1] - width :]
    return jnp.concatenate(
        [
            lax.ppermute(tail, axis, [(i, i + 1) for i in range(ends)]),
            cells,
            lax.ppermute(head, axis, [(i + 1, i) for i in range(ends)]),
        ],
        axis=1,
    )


def butterfly_sum(value, axis):
    count = lax.axis_size(axis)
    if count & (count - 1):
        return lax.psum(value, axis)
    bit = 1
    while bit < count:
        value = value + lax.ppermute(value, axis, [(i, i ^ bit) for i in range(count)])
        bit *= 2
    return value


def both_halves(value, axis):
    other = lax.ppermute(value, axis, [(0, 1), (1, 0)])
    first = lax.axis_index(axis) == 0
    return jnp.where(first, jnp.concatenate([value, other]), jnp.concatenate([other, value]))


def advance(values_in, coeffs, inside, step_size, forcing):
    middle = values_in[:, 1:-1, :]
    above_row = values_in[:, :-2, :]
    below_row = values_in[:, 2:, :]
    west_cell = jnp.pad(middle[:, :, :-1], ((0, 0), (0, 0), (1, 0)))
    east_cell = jnp.pad(middle[:, :, 1:], ((0, 0), (0, 0), (0, 1)))
    spread_term = coeffs[0] * (above_row + below_row + west_cell + east_cell - 4.0 * middle)
    tendency = (
        spread_term
        - coeffs[1] * (east_cell - west_cell) * 0.5
        - coeffs[2] * (below_row - above_row) * 0.5
    )
    if forcing is not None:
        tendency = tendency + forcing
    return (middle + step_size * tendency) * inside


def per_device(
    start_states,
    velocity_x,
    velocity_y,
    diffusivity,
    source_shape,
    params,
    obs_cell,
    obs_data,
    obs_noise,
    obs_var,
):
    coarse_dt = FINE_DT * FINE
    state = start_states[0]
    members_here, row_count, col_count = state.shape
    slabs = row_count * lax.axis_size("space")
    first_row = lax.axis_index("space") * row_count
    slice_index = lax.axis_index("tm")
    slices = lax.axis_size("tm")
    links = slices - 1
    depth = FINE + links
    group = members_here // slices
    band_width = col_count // params.shape[1]

    mine = lax.all_to_all(
        state.reshape(slices, group, row_count, col_count), "tm", 0, 0, tiled=True
    ).reshape(slices * group, row_count, col_count)
    my_params = lax.dynamic_slice_in_dim(params, slice_index * group, group, 0)
    spread_params = jnp.repeat(my_params, band_width, axis=1)

    fields = jnp.stack([diffusivity, velocity_x, velocity_y, source_shape])
    wide = with_halo(jnp.concatenate([mine, fields]), "space", depth)
    count = slices * group
    wide_state = wide[:count]
    wide_coeffs = wide[count : count + 3]
    wide_forcing = jnp.tile(wide[count + 3][None] * spread_params[:, None, :], (slices, 1, 1))
    global_rows = first_row - depth + jnp.arange(row_count + 2 * depth, dtype=jnp.int32)
    wide_inside = ((global_rows >= 0) & (global_rows < slabs)).astype(jnp.float32)[:, None]

    def step(values, low, step_size, forcing):
        n = values.shape[1]
        lo, hi = low + 1, low + n - 1
        q = None if forcing is None else forcing[:, lo:hi]
        return advance(values, wide_coeffs[:, lo:hi], wide_inside[lo:hi], step_size, q)

    current = wide_state
    coarse_part = step(wide_state, 0, coarse_dt, None)
    for section in range(FINE):
        current = step(current, section, FINE_DT, wide_forcing)
    coarse_part = coarse_part[:, FINE - 1 : FINE - 1 + current.shape[1]]
    fine = current.reshape(slices, group, -1, col_count)
    coarse_part = coarse_part.reshape(slices, group, -1, col_count)
    running = fine[0]
    results = [running[:, links : links + row_count]]
    for link in range(1, slices):
        correction = fine[link] - coarse_part[link]
        stepped = step(running, FINE + link - 1, coarse_dt, None)
        running = correction[:, link : correction.shape[1] - link] + stepped
        results.append(running[:, links - link : links - link + row_count])
    done = jnp.stack(results)
    running = lax.all_to_all(done, "tm", 0, 0, tiled=True).reshape(
        members_here, row_count, col_count
    )
    new_states = running[None]

    local_cell = obs_cell[0] - first_row * col_count
    rows = local_cell // col_count
    cols = local_cell % col_count
    picked_rows = jnp.take(running, rows, axis=1)
    at_col = lax.broadcasted_iota(jnp.int32, picked_rows.shape, 2) == cols[None, :, None]
    predicted = jnp.sum(jnp.where(at_col, picked_rows, 0.0), axis=2)
    every_pred = both_halves(predicted, "ens")
    every_param = both_halves(params, "ens")
    total = every_pred.shape[0]
    norm_factor = 1.0 / math.sqrt(total - 1)
    inv_spread = lax.rsqrt(obs_var[0])[None, :]
    pred_mean = jnp.mean(every_pred, axis=0, keepdims=True)
    anomaly = (every_pred - pred_mean) * (inv_spread * norm_factor)
    misfit = (obs_data[0][None, :] + obs_noise[0].T - every_pred) * inv_spread
    gram = jnp.dot(anomaly, anomaly.T, precision=lax.Precision.HIGHEST)
    cross = jnp.dot(anomaly, misfit.T, precision=lax.Precision.HIGHEST)
    sums = jnp.stack([gram, cross])
    sums = butterfly_sum(sums, "tm")
    sums = butterfly_sum(sums, "space")
    gram, cross = sums[0], sums[1]
    system = jnp.eye(total, dtype=jnp.float32) + gram
    factor = jnp.linalg.cholesky(system)
    weights = jax.scipy.linalg.cho_solve((factor, True), cross)
    param_anom = every_param - jnp.mean(every_param, axis=0)
    own_weights = lax.dynamic_slice_in_dim(
        weights, lax.axis_index("ens") * members_here, members_here, 1
    )
    new_params = (
        params + jnp.dot(own_weights.T, param_anom, precision=lax.Precision.HIGHEST) * norm_factor
    )
    return (new_states, new_params)


def solution(mesh):
    in_specs = (
        P("tm", "ens", "space", None),
        P("space", None),
        P("space", None),
        P("space", None),
        P("space", None),
        P("ens", None),
        P("tm", "space"),
        P("tm", "space"),
        P("tm", "space", None),
        P("tm", "space"),
    )
    out_specs = (P("tm", "ens", "space", None), P("ens", None))
    return jax.shard_map(
        per_device, mesh=mesh, in_specs=in_specs, out_specs=out_specs, check_vma=False
    )
```

```python
import math

import jax
import jax.numpy as jnp
from jax import lax
from jax.sharding import PartitionSpec as P

FINE = 4


FINE_DT = 0.25


def with_halo(cells, axis, width):
    count = lax.axis_size(axis)
    ends = count - 1
    head = cells[:, :width]
    tail = cells[:, cells.shape[1] - width :]
    return jnp.concatenate(
        [
            lax.ppermute(tail, axis, [(i, i + 1) for i in range(ends)]),
            cells,
            lax.ppermute(head, axis, [(i + 1, i) for i in range(ends)]),
        ],
        axis=1,
    )


def quad_sum(value, axis):
    count = lax.axis_size(axis)
    if count & (count - 1):
        return lax.psum(value, axis)
    bit = 1
    while bit < count:
        if bit * 4 <= count:
            near, far, both = (
                lax.ppermute(value, axis, [(i, i ^ (k * bit)) for i in range(count)])
                for k in (1, 2, 3)
            )
            value = (value + near) + (far + both)
            bit *= 4
        else:
            value = value + lax.ppermute(value, axis, [(i, i ^ bit) for i in range(count)])
            bit *= 2
    return value


def by_source(pieces, axis):
    count = lax.axis_size(axis)
    stacked = jnp.stack(pieces)
    order = (lax.axis_index(axis) - jnp.arange(count)) % count
    return jnp.take(stacked, order, axis=0)


def gather_axis(value, axis):
    count = lax.axis_size(axis)
    pieces = [value] + [
        lax.ppermute(value, axis, [(i, (i + d) % count) for i in range(count)])
        for d in range(1, count)
    ]
    return by_source(pieces, axis)


def exchange_axis(values, axis):
    count = lax.axis_size(axis)
    own = lax.axis_index(axis)
    pieces = [jnp.take(values, own, axis=0)] + [
        lax.ppermute(
            jnp.take(values, (own + d) % count, axis=0),
            axis,
            [(i, (i + d) % count) for i in range(count)],
        )
        for d in range(1, count)
    ]
    return by_source(pieces, axis)


def both_halves(value, axis):
    other = lax.ppermute(value, axis, [(0, 1), (1, 0)])
    first = lax.axis_index(axis) == 0
    return jnp.where(first, jnp.concatenate([value, other]), jnp.concatenate([other, value]))


def advance(values_in, coeffs, inside, step_size, forcing):
    middle = values_in[:, 1:-1, :]
    above_row = values_in[:, :-2, :]
    below_row = values_in[:, 2:, :]
    west_cell = jnp.pad(middle[:, :, :-1], ((0, 0), (0, 0), (1, 0)))
    east_cell = jnp.pad(middle[:, :, 1:], ((0, 0), (0, 0), (0, 1)))
    spread_term = coeffs[0] * (above_row + below_row + west_cell + east_cell - 4.0 * middle)
    tendency = (
        spread_term
        - coeffs[1] * (east_cell - west_cell) * 0.5
        - coeffs[2] * (below_row - above_row) * 0.5
    )
    if forcing is not None:
        tendency = tendency + forcing
    return (middle + step_size * tendency) * inside


def per_device(
    start_states,
    velocity_x,
    velocity_y,
    diffusivity,
    source_shape,
    params,
    obs_cell,
    obs_data,
    obs_noise,
    obs_var,
):
    coarse_dt = FINE_DT * FINE
    state = start_states[0]
    members_here, row_count, col_count = state.shape
    slabs = row_count * lax.axis_size("space")
    first_row = lax.axis_index("space") * row_count
    slice_index = lax.axis_index("tm")
    slices = lax.axis_size("tm")
    links = slices - 1
    depth = FINE + links
    group = members_here // slices
    band_width = col_count // params.shape[1]

    fields = jnp.stack([diffusivity, velocity_x, velocity_y, source_shape])
    wide_fields = with_halo(fields, "space", depth)
    every_cell = gather_axis(obs_cell[0], "tm")
    every_param = both_halves(params, "ens")

    mine = lax.all_to_all(
        state.reshape(slices, group, row_count, col_count), "tm", 0, 0, tiled=True
    ).reshape(slices * group, row_count, col_count)
    my_params = lax.dynamic_slice_in_dim(params, slice_index * group, group, 0)
    spread_params = jnp.repeat(my_params, band_width, axis=1)

    wide_state = with_halo(mine, "space", depth)
    wide_coeffs = wide_fields[:3]
    wide_forcing = jnp.tile(wide_fields[3][None] * spread_params[:, None, :], (slices, 1, 1))
    global_rows = first_row - depth + jnp.arange(row_count + 2 * depth, dtype=jnp.int32)
    wide_inside = ((global_rows >= 0) & (global_rows < slabs)).astype(jnp.float32)[:, None]

    def step(values, low, step_size, forcing):
        n = values.shape[1]
        lo, hi = low + 1, low + n - 1
        q = None if forcing is None else forcing[:, lo:hi]
        return advance(values, wide_coeffs[:, lo:hi], wide_inside[lo:hi], step_size, q)

    current = wide_state
    coarse_part = step(wide_state, 0, coarse_dt, None)
    for section in range(FINE):
        current = step(current, section, FINE_DT, wide_forcing)
    coarse_part = coarse_part[:, FINE - 1 : FINE - 1 + current.shape[1]]
    fine = current.reshape(slices, group, -1, col_count)
    coarse_part = coarse_part.reshape(slices, group, -1, col_count)
    running = fine[0]
    results = [running[:, links : links + row_count]]
    for link in range(1, slices):
        correction = fine[link] - coarse_part[link]
        stepped = step(running, FINE + link - 1, coarse_dt, None)
        running = correction[:, link : correction.shape[1] - link] + stepped
        results.append(running[:, links - link : links - link + row_count])
    done = jnp.stack(results)
    running = lax.all_to_all(done, "tm", 0, 0, tiled=True).reshape(
        members_here, row_count, col_count
    )
    new_states = running[None]

    local_cell = every_cell - first_row * col_count
    rows = local_cell // col_count
    cols = local_cell % col_count
    picked_rows = jnp.take_along_axis(done, rows[:, None, :, None], axis=2)
    at_col = lax.broadcasted_iota(jnp.int32, picked_rows.shape, 3) == cols[:, None, :, None]
    local_pred = jnp.sum(jnp.where(at_col, picked_rows, 0.0), axis=3)
    predicted = exchange_axis(local_pred, "tm").reshape(members_here, -1)
    every_pred = both_halves(predicted, "ens")
    total = every_pred.shape[0]
    norm_factor = 1.0 / math.sqrt(total - 1)
    inv_spread = lax.rsqrt(obs_var[0])[None, :]
    pred_mean = jnp.mean(every_pred, axis=0, keepdims=True)
    anomaly = (every_pred - pred_mean) * (inv_spread * norm_factor)
    misfit = (obs_data[0][None, :] + obs_noise[0].T - every_pred) * inv_spread
    gram = jnp.dot(anomaly, anomaly.T, precision=lax.Precision.HIGHEST)
    cross = jnp.dot(anomaly, misfit.T, precision=lax.Precision.HIGHEST)
    sums = jnp.stack([gram, cross])
    sums = quad_sum(sums, "tm")
    sums = quad_sum(sums, "space")
    gram, cross = sums[0], sums[1]
    system = jnp.eye(total, dtype=jnp.float32) + gram
    factor = jnp.linalg.cholesky(system)
    weights = jax.scipy.linalg.cho_solve((factor, True), cross)
    param_anom = every_param - jnp.mean(every_param, axis=0)
    own_weights = lax.dynamic_slice_in_dim(
        weights, lax.axis_index("ens") * members_here, members_here, 1
    )
    new_params = (
        params + jnp.dot(own_weights.T, param_anom, precision=lax.Precision.HIGHEST) * norm_factor
    )
    return (new_states, new_params)


def solution(mesh):
    in_specs = (
        P("tm", "ens", "space", None),
        P("space", None),
        P("space", None),
        P("space", None),
        P("space", None),
        P("ens", None),
        P("tm", "space"),
        P("tm", "space"),
        P("tm", "space", None),
        P("tm", "space"),
    )
    out_specs = (P("tm", "ens", "space", None), P("ens", None))
    return jax.shard_map(
        per_device, mesh=mesh, in_specs=in_specs, out_specs=out_specs, check_vma=False
    )
```

```python
import math

import jax
import jax.numpy as jnp
from jax import lax
from jax.sharding import PartitionSpec as P

FINE = 4


FINE_DT = 0.25


def with_halo(cells, axis, width):
    count = lax.axis_size(axis)
    ends = count - 1
    head = cells[:, :width]
    tail = cells[:, cells.shape[1] - width :]
    return jnp.concatenate(
        [
            lax.ppermute(tail, axis, [(i, i + 1) for i in range(ends)]),
            cells,
            lax.ppermute(head, axis, [(i + 1, i) for i in range(ends)]),
        ],
        axis=1,
    )


def quad_sum(value, axis):
    count = lax.axis_size(axis)
    if count & (count - 1):
        return lax.psum(value, axis)
    bit = 1
    while bit < count:
        if bit * 4 <= count:
            near, far, both = (
                lax.ppermute(value, axis, [(i, i ^ (k * bit)) for i in range(count)])
                for k in (1, 2, 3)
            )
            value = (value + near) + (far + both)
            bit *= 4
        else:
            value = value + lax.ppermute(value, axis, [(i, i ^ bit) for i in range(count)])
            bit *= 2
    return value


def by_source(pieces, axis):
    count = lax.axis_size(axis)
    stacked = jnp.stack(pieces)
    order = (lax.axis_index(axis) - jnp.arange(count)) % count
    return jnp.take(stacked, order, axis=0)


def gather_axis(value, axis):
    count = lax.axis_size(axis)
    pieces = [value] + [
        lax.ppermute(value, axis, [(i, (i + d) % count) for i in range(count)])
        for d in range(1, count)
    ]
    return by_source(pieces, axis)


def exchange_axis(values, axis):
    count = lax.axis_size(axis)
    own = lax.axis_index(axis)
    pieces = [jnp.take(values, own, axis=0)] + [
        lax.ppermute(
            jnp.take(values, (own + d) % count, axis=0),
            axis,
            [(i, (i + d) % count) for i in range(count)],
        )
        for d in range(1, count)
    ]
    return by_source(pieces, axis)


def spread_axis(values, axis):
    count = lax.axis_size(axis)
    if count != 4:
        return lax.all_to_all(values, axis, 0, 0, tiled=True)
    own = lax.axis_index(axis)

    def shift(value, d):
        return lax.ppermute(value, axis, [(i, (i + d) % count) for i in range(count)])

    def bound_for(d):
        return jnp.take(values, (own + d) % count, axis=0)

    far = bound_for(2)
    half = far.shape[1] // 2
    far_direct = shift(far[:, :half], 2)
    far_relayed = shift(shift(far[:, half:], -1), -1)
    pieces = [
        bound_for(0),
        shift(bound_for(1), 1),
        jnp.concatenate([far_direct, far_relayed], axis=1),
        shift(bound_for(3), 3),
    ]
    return by_source(pieces, axis)


def both_halves(value, axis):
    other = lax.ppermute(value, axis, [(0, 1), (1, 0)])
    first = lax.axis_index(axis) == 0
    return jnp.where(first, jnp.concatenate([value, other]), jnp.concatenate([other, value]))


def advance(values_in, coeffs, inside, step_size, forcing):
    middle = values_in[:, 1:-1, :]
    above_row = values_in[:, :-2, :]
    below_row = values_in[:, 2:, :]
    west_cell = jnp.pad(middle[:, :, :-1], ((0, 0), (0, 0), (1, 0)))
    east_cell = jnp.pad(middle[:, :, 1:], ((0, 0), (0, 0), (0, 1)))
    spread_term = coeffs[0] * (above_row + below_row + west_cell + east_cell - 4.0 * middle)
    tendency = (
        spread_term
        - coeffs[1] * (east_cell - west_cell) * 0.5
        - coeffs[2] * (below_row - above_row) * 0.5
    )
    if forcing is not None:
        tendency = tendency + forcing
    return (middle + step_size * tendency) * inside


def per_device(
    start_states,
    velocity_x,
    velocity_y,
    diffusivity,
    source_shape,
    params,
    obs_cell,
    obs_data,
    obs_noise,
    obs_var,
):
    coarse_dt = FINE_DT * FINE
    state = start_states[0]
    members_here, row_count, col_count = state.shape
    slabs = row_count * lax.axis_size("space")
    first_row = lax.axis_index("space") * row_count
    slice_index = lax.axis_index("tm")
    slices = lax.axis_size("tm")
    links = slices - 1
    depth = FINE + links
    group = members_here // slices
    band_width = col_count // params.shape[1]

    fields = jnp.stack([diffusivity, velocity_x, velocity_y, source_shape])
    wide_fields = with_halo(fields, "space", depth)
    every_cell = gather_axis(obs_cell[0], "tm")
    every_param = both_halves(params, "ens")

    mine = spread_axis(state.reshape(slices, group, row_count, col_count), "tm").reshape(
        slices * group, row_count, col_count
    )
    my_params = lax.dynamic_slice_in_dim(params, slice_index * group, group, 0)
    spread_params = jnp.repeat(my_params, band_width, axis=1)

    wide_state = with_halo(mine, "space", depth)
    wide_coeffs = wide_fields[:3]
    wide_forcing = jnp.tile(wide_fields[3][None] * spread_params[:, None, :], (slices, 1, 1))
    global_rows = first_row - depth + jnp.arange(row_count + 2 * depth, dtype=jnp.int32)
    wide_inside = ((global_rows >= 0) & (global_rows < slabs)).astype(jnp.float32)[:, None]

    def step(values, low, step_size, forcing):
        n = values.shape[1]
        lo, hi = low + 1, low + n - 1
        q = None if forcing is None else forcing[:, lo:hi]
        return advance(values, wide_coeffs[:, lo:hi], wide_inside[lo:hi], step_size, q)

    current = wide_state
    coarse_part = step(wide_state, 0, coarse_dt, None)
    for section in range(FINE):
        current = step(current, section, FINE_DT, wide_forcing)
    coarse_part = coarse_part[:, FINE - 1 : FINE - 1 + current.shape[1]]
    fine = current.reshape(slices, group, -1, col_count)
    coarse_part = coarse_part.reshape(slices, group, -1, col_count)
    running = fine[0]
    results = [running[:, links : links + row_count]]
    for link in range(1, slices):
        correction = fine[link] - coarse_part[link]
        stepped = step(running, FINE + link - 1, coarse_dt, None)
        running = correction[:, link : correction.shape[1] - link] + stepped
        results.append(running[:, links - link : links - link + row_count])
    done = jnp.stack(results)
    running = spread_axis(done, "tm").reshape(
        members_here, row_count, col_count
    )
    new_states = running[None]

    local_cell = every_cell - first_row * col_count
    rows = local_cell // col_count
    cols = local_cell % col_count
    picked_rows = jnp.take_along_axis(done, rows[:, None, :, None], axis=2)
    at_col = lax.broadcasted_iota(jnp.int32, picked_rows.shape, 3) == cols[:, None, :, None]
    local_pred = jnp.sum(jnp.where(at_col, picked_rows, 0.0), axis=3)
    predicted = exchange_axis(local_pred, "tm").reshape(members_here, -1)
    every_pred = both_halves(predicted, "ens")
    total = every_pred.shape[0]
    norm_factor = 1.0 / math.sqrt(total - 1)
    inv_spread = lax.rsqrt(obs_var[0])[None, :]
    pred_mean = jnp.mean(every_pred, axis=0, keepdims=True)
    anomaly = (every_pred - pred_mean) * (inv_spread * norm_factor)
    misfit = (obs_data[0][None, :] + obs_noise[0].T - every_pred) * inv_spread
    gram = jnp.dot(anomaly, anomaly.T, precision=lax.Precision.HIGHEST)
    cross = jnp.dot(anomaly, misfit.T, precision=lax.Precision.HIGHEST)
    sums = jnp.stack([gram, cross])
    sums = quad_sum(sums, "tm")
    sums = quad_sum(sums, "space")
    gram, cross = sums[0], sums[1]
    system = jnp.eye(total, dtype=jnp.float32) + gram
    factor = jnp.linalg.cholesky(system)
    weights = jax.scipy.linalg.cho_solve((factor, True), cross)
    param_anom = every_param - jnp.mean(every_param, axis=0)
    own_weights = lax.dynamic_slice_in_dim(
        weights, lax.axis_index("ens") * members_here, members_here, 1
    )
    new_params = (
        params + jnp.dot(own_weights.T, param_anom, precision=lax.Precision.HIGHEST) * norm_factor
    )
    return (new_states, new_params)


def solution(mesh):
    in_specs = (
        P("tm", "ens", "space", None),
        P("space", None),
        P("space", None),
        P("space", None),
        P("space", None),
        P("ens", None),
        P("tm", "space"),
        P("tm", "space"),
        P("tm", "space", None),
        P("tm", "space"),
    )
    out_specs = (P("tm", "ens", "space", None), P("ens", None))
    return jax.shard_map(
        per_device, mesh=mesh, in_specs=in_specs, out_specs=out_specs, check_vma=False
    )
```

```python
import math

import jax
import jax.numpy as jnp
from jax import lax
from jax.sharding import PartitionSpec as P

FINE = 4


FINE_DT = 0.25


def with_halo(cells, axis, width):
    count = lax.axis_size(axis)
    ends = count - 1
    head = cells[:, :width]
    tail = cells[:, cells.shape[1] - width :]
    return jnp.concatenate(
        [
            lax.ppermute(tail, axis, [(i, i + 1) for i in range(ends)]),
            cells,
            lax.ppermute(head, axis, [(i + 1, i) for i in range(ends)]),
        ],
        axis=1,
    )


def quad_sum(value, axis):
    count = lax.axis_size(axis)
    if count & (count - 1):
        return lax.psum(value, axis)
    bit = 1
    while bit < count:
        if bit * 4 <= count:
            near, far, both = (
                lax.ppermute(value, axis, [(i, i ^ (k * bit)) for i in range(count)])
                for k in (1, 2, 3)
            )
            value = (value + near) + (far + both)
            bit *= 4
        else:
            value = value + lax.ppermute(value, axis, [(i, i ^ bit) for i in range(count)])
            bit *= 2
    return value


def by_source(pieces, axis):
    count = lax.axis_size(axis)
    stacked = jnp.stack(pieces)
    order = (lax.axis_index(axis) - jnp.arange(count)) % count
    return jnp.take(stacked, order, axis=0)


def gather_axis(value, axis):
    count = lax.axis_size(axis)
    pieces = [value] + [
        lax.ppermute(value, axis, [(i, (i + d) % count) for i in range(count)])
        for d in range(1, count)
    ]
    return by_source(pieces, axis)


def both_halves(value, axis):
    other = lax.ppermute(value, axis, [(0, 1), (1, 0)])
    first = lax.axis_index(axis) == 0
    return jnp.where(first, jnp.concatenate([value, other]), jnp.concatenate([other, value]))


def advance(values_in, coeffs, inside, step_size, forcing):
    middle = values_in[:, 1:-1, :]
    above_row = values_in[:, :-2, :]
    below_row = values_in[:, 2:, :]
    west_cell = jnp.pad(middle[:, :, :-1], ((0, 0), (0, 0), (1, 0)))
    east_cell = jnp.pad(middle[:, :, 1:], ((0, 0), (0, 0), (0, 1)))
    spread_term = coeffs[0] * (above_row + below_row + west_cell + east_cell - 4.0 * middle)
    tendency = (
        spread_term
        - coeffs[1] * (east_cell - west_cell) * 0.5
        - coeffs[2] * (below_row - above_row) * 0.5
    )
    if forcing is not None:
        tendency = tendency + forcing
    return (middle + step_size * tendency) * inside


def per_device(
    start_states,
    velocity_x,
    velocity_y,
    diffusivity,
    source_shape,
    params,
    obs_cell,
    obs_data,
    obs_noise,
    obs_var,
):
    coarse_dt = FINE_DT * FINE
    state = start_states[0]
    members_here, row_count, col_count = state.shape
    slabs = row_count * lax.axis_size("space")
    first_row = lax.axis_index("space") * row_count
    slice_index = lax.axis_index("tm")
    slices = lax.axis_size("tm")
    links = slices - 1
    depth = FINE + links
    group = members_here // slices
    band_width = col_count // params.shape[1]

    fields = jnp.stack([diffusivity, velocity_x, velocity_y, source_shape])
    wide_fields = with_halo(fields, "space", depth)
    obs_pack = jnp.concatenate(
        [
            obs_cell[0].astype(jnp.float32)[:, None],
            obs_data[0][:, None],
            obs_var[0][:, None],
            obs_noise[0],
        ],
        axis=1,
    )
    every_obs = gather_axis(obs_pack, "tm")
    every_cell = every_obs[:, :, 0].astype(jnp.int32)
    every_obs = every_obs[:, :, 1:]
    every_data = every_obs[:, :, 0]
    every_var = every_obs[:, :, 1]
    every_noise = every_obs[:, :, 2:]
    every_param = both_halves(params, "ens")

    mine = lax.all_to_all(
        state.reshape(slices, group, row_count, col_count), "tm", 0, 0, tiled=True
    ).reshape(slices * group, row_count, col_count)
    my_params = lax.dynamic_slice_in_dim(params, slice_index * group, group, 0)
    spread_params = jnp.repeat(my_params, band_width, axis=1)

    wide_state = with_halo(mine, "space", depth)
    wide_coeffs = wide_fields[:3]
    wide_forcing = jnp.tile(wide_fields[3][None] * spread_params[:, None, :], (slices, 1, 1))
    global_rows = first_row - depth + jnp.arange(row_count + 2 * depth, dtype=jnp.int32)
    wide_inside = ((global_rows >= 0) & (global_rows < slabs)).astype(jnp.float32)[:, None]

    def step(values, low, step_size, forcing):
        n = values.shape[1]
        lo, hi = low + 1, low + n - 1
        q = None if forcing is None else forcing[:, lo:hi]
        return advance(values, wide_coeffs[:, lo:hi], wide_inside[lo:hi], step_size, q)

    current = wide_state
    coarse_part = step(wide_state, 0, coarse_dt, None)
    for section in range(FINE):
        current = step(current, section, FINE_DT, wide_forcing)
    coarse_part = coarse_part[:, FINE - 1 : FINE - 1 + current.shape[1]]
    fine = current.reshape(slices, group, -1, col_count)
    coarse_part = coarse_part.reshape(slices, group, -1, col_count)
    running = fine[0]
    results = [running[:, links : links + row_count]]
    for link in range(1, slices):
        correction = fine[link] - coarse_part[link]
        stepped = step(running, FINE + link - 1, coarse_dt, None)
        running = correction[:, link : correction.shape[1] - link] + stepped
        results.append(running[:, links - link : links - link + row_count])
    done = jnp.stack(results)
    running = lax.all_to_all(done, "tm", 0, 0, tiled=True).reshape(
        members_here, row_count, col_count
    )
    new_states = running[None]

    local_cell = every_cell - first_row * col_count
    rows = local_cell // col_count
    cols = local_cell % col_count
    picked_rows = jnp.take_along_axis(done, rows[:, None, :, None], axis=2)
    at_col = lax.broadcasted_iota(jnp.int32, picked_rows.shape, 3) == cols[:, None, :, None]
    local_pred = jnp.sum(jnp.where(at_col, picked_rows, 0.0), axis=3)
    pred = gather_axis(local_pred, "tm")
    pred = jnp.transpose(pred, (0, 2, 1, 3)).reshape(members_here, -1)
    every_pred = both_halves(pred, "ens")
    total = every_pred.shape[0]
    norm_factor = 1.0 / math.sqrt(total - 1)
    inv_spread = lax.rsqrt(every_var).reshape(1, -1)
    pred_mean = jnp.mean(every_pred, axis=0, keepdims=True)
    anomaly = (every_pred - pred_mean) * (inv_spread * norm_factor)
    noise = jnp.transpose(every_noise, (2, 0, 1)).reshape(total, -1)
    misfit = (every_data.reshape(1, -1) + noise - every_pred) * inv_spread
    gram = jnp.dot(anomaly, anomaly.T, precision=lax.Precision.HIGHEST)
    cross = jnp.dot(anomaly, misfit.T, precision=lax.Precision.HIGHEST)
    sums = jnp.stack([gram, cross])
    sums = quad_sum(sums, "space")
    gram, cross = sums[0], sums[1]
    system = jnp.eye(total, dtype=jnp.float32) + gram
    factor = jnp.linalg.cholesky(system)
    weights = jax.scipy.linalg.cho_solve((factor, True), cross)
    param_anom = every_param - jnp.mean(every_param, axis=0)
    own_weights = lax.dynamic_slice_in_dim(
        weights, lax.axis_index("ens") * members_here, members_here, 1
    )
    new_params = (
        params + jnp.dot(own_weights.T, param_anom, precision=lax.Precision.HIGHEST) * norm_factor
    )
    return (new_states, new_params)


def solution(mesh):
    in_specs = (
        P("tm", "ens", "space", None),
        P("space", None),
        P("space", None),
        P("space", None),
        P("space", None),
        P("ens", None),
        P("tm", "space"),
        P("tm", "space"),
        P("tm", "space", None),
        P("tm", "space"),
    )
    out_specs = (P("tm", "ens", "space", None), P("ens", None))
    return jax.shard_map(
        per_device, mesh=mesh, in_specs=in_specs, out_specs=out_specs, check_vma=False
    )
```

```python
import math

import jax
import jax.numpy as jnp
from jax import lax
from jax.sharding import PartitionSpec as P

FINE = 4


FINE_DT = 0.25


def with_halo(cells, axis, width):
    count = lax.axis_size(axis)
    ends = count - 1
    head = cells[:, :width]
    tail = cells[:, cells.shape[1] - width :]
    return jnp.concatenate(
        [
            lax.ppermute(tail, axis, [(i, i + 1) for i in range(ends)]),
            cells,
            lax.ppermute(head, axis, [(i + 1, i) for i in range(ends)]),
        ],
        axis=1,
    )


def quad_sum(value, axis):
    count = lax.axis_size(axis)
    if count & (count - 1):
        return lax.psum(value, axis)
    bit = 1
    while bit < count:
        if bit * 4 <= count:
            near, far, both = (
                lax.ppermute(value, axis, [(i, i ^ (k * bit)) for i in range(count)])
                for k in (1, 2, 3)
            )
            value = (value + near) + (far + both)
            bit *= 4
        else:
            value = value + lax.ppermute(value, axis, [(i, i ^ bit) for i in range(count)])
            bit *= 2
    return value


def by_source(pieces, axis):
    count = lax.axis_size(axis)
    stacked = jnp.stack(pieces)
    order = (lax.axis_index(axis) - jnp.arange(count)) % count
    return jnp.take(stacked, order, axis=0)


def gather_axis(value, axis):
    count = lax.axis_size(axis)
    pieces = [value] + [
        lax.ppermute(value, axis, [(i, (i + d) % count) for i in range(count)])
        for d in range(1, count)
    ]
    return by_source(pieces, axis)


def both_halves(value, axis):
    other = lax.ppermute(value, axis, [(0, 1), (1, 0)])
    first = lax.axis_index(axis) == 0
    return jnp.where(first, jnp.concatenate([value, other]), jnp.concatenate([other, value]))


def advance(values_in, coeffs, inside, step_size, forcing):
    middle = values_in[..., 1:-1, :]
    above_row = values_in[..., :-2, :]
    below_row = values_in[..., 2:, :]
    edge = [(0, 0)] * (values_in.ndim - 1)
    west_cell = jnp.pad(middle[..., :-1], edge + [(1, 0)])
    east_cell = jnp.pad(middle[..., 1:], edge + [(0, 1)])
    spread_term = coeffs[0] * (above_row + below_row + west_cell + east_cell - 4.0 * middle)
    tendency = (
        spread_term
        - coeffs[1] * (east_cell - west_cell) * 0.5
        - coeffs[2] * (below_row - above_row) * 0.5
    )
    if forcing is not None:
        tendency = tendency + forcing
    return (middle + step_size * tendency) * inside


def per_device(
    start_states,
    velocity_x,
    velocity_y,
    diffusivity,
    source_shape,
    params,
    obs_cell,
    obs_data,
    obs_noise,
    obs_var,
):
    coarse_dt = FINE_DT * FINE
    state = start_states[0]
    members_here, row_count, col_count = state.shape
    slabs = row_count * lax.axis_size("space")
    first_row = lax.axis_index("space") * row_count
    slice_index = lax.axis_index("tm")
    slices = lax.axis_size("tm")
    links = slices - 1
    depth = FINE + links
    group = members_here // slices
    band_width = col_count // params.shape[1]

    every_param = both_halves(params, "ens")
    obs_pack = jnp.concatenate(
        [
            obs_cell[0].astype(jnp.float32)[:, None],
            obs_data[0][:, None],
            obs_var[0][:, None],
            obs_noise[0],
        ],
        axis=1,
    )
    every_obs = gather_axis(obs_pack, "tm")
    every_cell = every_obs[:, :, 0].astype(jnp.int32)
    every_obs = every_obs[:, :, 1:]
    every_data = every_obs[:, :, 0]
    every_var = every_obs[:, :, 1]
    every_noise = every_obs[:, :, 2:]

    fields = jnp.stack([diffusivity, velocity_x, velocity_y, source_shape])
    wide = with_halo(jnp.concatenate([state, fields]), "space", depth)
    wide_coeffs = wide[members_here : members_here + 3]
    wide_state = lax.all_to_all(
        wide[:members_here].reshape(slices, group, row_count + 2 * depth, col_count),
        "tm",
        0,
        0,
        tiled=True,
    )
    my_params = lax.dynamic_slice_in_dim(params, slice_index * group, group, 0)
    spread_params = jnp.repeat(my_params, band_width, axis=1)
    wide_forcing = wide[members_here + 3][None] * spread_params[:, None, :]
    global_rows = first_row - depth + jnp.arange(row_count + 2 * depth, dtype=jnp.int32)
    wide_inside = ((global_rows >= 0) & (global_rows < slabs)).astype(jnp.float32)[:, None]

    def step(values, low, step_size, forcing):
        n = values.shape[-2]
        lo, hi = low + 1, low + n - 1
        q = None if forcing is None else forcing[:, lo:hi]
        return advance(values, wide_coeffs[:, lo:hi], wide_inside[lo:hi], step_size, q)

    current = wide_state
    coarse_part = step(wide_state, 0, coarse_dt, None)
    for section in range(FINE):
        current = step(current, section, FINE_DT, wide_forcing)
    fine = current
    coarse_part = coarse_part[:, :, FINE - 1 : FINE - 1 + current.shape[2]]
    running = fine[0]
    results = [running[:, links : links + row_count]]
    for link in range(1, slices):
        correction = fine[link] - coarse_part[link]
        stepped = step(running, FINE + link - 1, coarse_dt, None)
        running = correction[:, link : correction.shape[1] - link] + stepped
        results.append(running[:, links - link : links - link + row_count])
    done = jnp.stack(results)
    running = lax.all_to_all(done, "tm", 0, 0, tiled=True).reshape(
        members_here, row_count, col_count
    )
    new_states = running[None]

    local_cell = every_cell - first_row * col_count
    rows = local_cell // col_count
    cols = local_cell % col_count
    at_slice = lax.broadcasted_iota(jnp.int32, (slices, group, rows.shape[1]), 0)
    at_member = lax.broadcasted_iota(jnp.int32, (slices, group, rows.shape[1]), 1)
    local_pred = done[at_slice, at_member, rows[:, None, :], cols[:, None, :]]
    pred = gather_axis(local_pred, "tm")
    pred = jnp.transpose(pred, (0, 2, 1, 3)).reshape(members_here, -1)
    every_pred = both_halves(pred, "ens")
    total = every_pred.shape[0]
    norm_factor = 1.0 / math.sqrt(total - 1)
    inv_spread = lax.rsqrt(every_var).reshape(1, -1)
    pred_mean = jnp.mean(every_pred, axis=0, keepdims=True)
    anomaly = (every_pred - pred_mean) * (inv_spread * norm_factor)
    noise = jnp.transpose(every_noise, (2, 0, 1)).reshape(total, -1)
    misfit = (every_data.reshape(1, -1) + noise - every_pred) * inv_spread
    gram = jnp.dot(anomaly, anomaly.T, precision=lax.Precision.HIGHEST)
    cross = jnp.dot(anomaly, misfit.T, precision=lax.Precision.HIGHEST)
    sums = jnp.stack([gram, cross])
    sums = quad_sum(sums, "space")
    gram, cross = sums[0], sums[1]
    system = jnp.eye(total, dtype=jnp.float32) + gram
    factor = jnp.linalg.cholesky(system)
    weights = jax.scipy.linalg.cho_solve((factor, True), cross)
    param_anom = every_param - jnp.mean(every_param, axis=0)
    own_weights = lax.dynamic_slice_in_dim(
        weights, lax.axis_index("ens") * members_here, members_here, 1
    )
    new_params = (
        params + jnp.dot(own_weights.T, param_anom, precision=lax.Precision.HIGHEST) * norm_factor
    )
    return (new_states, new_params)


def solution(mesh):
    in_specs = (
        P("tm", "ens", "space", None),
        P("space", None),
        P("space", None),
        P("space", None),
        P("space", None),
        P("ens", None),
        P("tm", "space"),
        P("tm", "space"),
        P("tm", "space", None),
        P("tm", "space"),
    )
    out_specs = (P("tm", "ens", "space", None), P("ens", None))
    return jax.shard_map(
        per_device, mesh=mesh, in_specs=in_specs, out_specs=out_specs, check_vma=False
    )
```

```python
import math

import jax
import jax.numpy as jnp
from jax import lax
from jax.sharding import PartitionSpec as P

FINE = 4


FINE_DT = 0.25


def with_halo(cells, axis, width):
    count = lax.axis_size(axis)
    ends = count - 1
    head = cells[:, :width]
    tail = cells[:, cells.shape[1] - width :]
    return jnp.concatenate(
        [
            lax.ppermute(tail, axis, [(i, i + 1) for i in range(ends)]),
            cells,
            lax.ppermute(head, axis, [(i + 1, i) for i in range(ends)]),
        ],
        axis=1,
    )


def both_halves(value, axis):
    other = lax.ppermute(value, axis, [(0, 1), (1, 0)])
    first = lax.axis_index(axis) == 0
    return jnp.where(first, jnp.concatenate([value, other]), jnp.concatenate([other, value]))


def advance(values_in, coeffs, inside, step_size, forcing):
    middle = values_in[:, 1:-1, :]
    above_row = values_in[:, :-2, :]
    below_row = values_in[:, 2:, :]
    west_cell = jnp.pad(middle[:, :, :-1], ((0, 0), (0, 0), (1, 0)))
    east_cell = jnp.pad(middle[:, :, 1:], ((0, 0), (0, 0), (0, 1)))
    spread_term = coeffs[0] * (above_row + below_row + west_cell + east_cell - 4.0 * middle)
    tendency = (
        spread_term
        - coeffs[1] * (east_cell - west_cell) * 0.5
        - coeffs[2] * (below_row - above_row) * 0.5
    )
    if forcing is not None:
        tendency = tendency + forcing
    return (middle + step_size * tendency) * inside


def per_device(
    start_states,
    velocity_x,
    velocity_y,
    diffusivity,
    source_shape,
    params,
    obs_cell,
    obs_data,
    obs_noise,
    obs_var,
):
    coarse_dt = FINE_DT * FINE
    state = start_states[0]
    members_here, row_count, col_count = state.shape
    slabs = row_count * lax.axis_size("space")
    first_row = lax.axis_index("space") * row_count
    slice_index = lax.axis_index("tm")
    slices = lax.axis_size("tm")
    links = slices - 1
    depth = FINE + links
    group = members_here // slices
    band_width = col_count // params.shape[1]

    mine = lax.all_to_all(
        state.reshape(slices, group, row_count, col_count), "tm", 0, 0, tiled=True
    ).reshape(slices * group, row_count, col_count)
    my_params = lax.dynamic_slice_in_dim(params, slice_index * group, group, 0)
    spread_params = jnp.repeat(my_params, band_width, axis=1)

    fields = jnp.stack([diffusivity, velocity_x, velocity_y, source_shape])
    wide = with_halo(jnp.concatenate([mine, fields]), "space", depth)
    count = slices * group
    wide_state = wide[:count]
    wide_coeffs = wide[count : count + 3]
    wide_forcing = jnp.tile(wide[count + 3][None] * spread_params[:, None, :], (slices, 1, 1))
    global_rows = first_row - depth + jnp.arange(row_count + 2 * depth, dtype=jnp.int32)
    wide_inside = ((global_rows >= 0) & (global_rows < slabs)).astype(jnp.float32)[:, None]

    def step(values, low, step_size, forcing):
        n = values.shape[1]
        lo, hi = low + 1, low + n - 1
        q = None if forcing is None else forcing[:, lo:hi]
        return advance(values, wide_coeffs[:, lo:hi], wide_inside[lo:hi], step_size, q)

    current = wide_state
    coarse_part = step(wide_state, 0, coarse_dt, None)
    for section in range(FINE):
        current = step(current, section, FINE_DT, wide_forcing)
    coarse_part = coarse_part[:, FINE - 1 : FINE - 1 + current.shape[1]]
    fine = current.reshape(slices, group, -1, col_count)
    coarse_part = coarse_part.reshape(slices, group, -1, col_count)
    running = fine[0]
    results = [running[:, links : links + row_count]]
    for link in range(1, slices):
        correction = fine[link] - coarse_part[link]
        stepped = step(running, FINE + link - 1, coarse_dt, None)
        running = correction[:, link : correction.shape[1] - link] + stepped
        results.append(running[:, links - link : links - link + row_count])
    done = jnp.stack(results)
    running = lax.all_to_all(done, "tm", 0, 0, tiled=True).reshape(
        members_here, row_count, col_count
    )
    new_states = running[None]

    local_cell = obs_cell[0] - first_row * col_count
    rows = local_cell // col_count
    cols = local_cell % col_count
    picked_rows = jnp.take(running, rows, axis=1)
    at_col = lax.broadcasted_iota(jnp.int32, picked_rows.shape, 2) == cols[None, :, None]
    predicted = jnp.sum(jnp.where(at_col, picked_rows, 0.0), axis=2)
    every_pred = both_halves(predicted, "ens")
    every_param = both_halves(params, "ens")
    total = every_pred.shape[0]
    norm_factor = 1.0 / math.sqrt(total - 1)
    inv_spread = lax.rsqrt(obs_var[0])[None, :]
    pred_mean = jnp.mean(every_pred, axis=0, keepdims=True)
    anomaly = (every_pred - pred_mean) * (inv_spread * norm_factor)
    misfit = (obs_data[0][None, :] + obs_noise[0].T - every_pred) * inv_spread
    half = anomaly.shape[1] // 2
    own_half = lax.axis_index("ens") * half
    part_anom = lax.dynamic_slice_in_dim(anomaly, own_half, half, 1)
    part_misfit = lax.dynamic_slice_in_dim(misfit, own_half, half, 1)
    gram = jnp.dot(part_anom, part_anom.T, precision=lax.Precision.HIGHEST)
    cross = jnp.dot(part_anom, part_misfit.T, precision=lax.Precision.HIGHEST)
    sums = lax.psum(jnp.stack([gram, cross]), ("tm", "space", "ens"))
    gram, cross = sums[0], sums[1]
    system = jnp.eye(total, dtype=jnp.float32) + gram
    factor = jnp.linalg.cholesky(system)
    weights = jax.scipy.linalg.cho_solve((factor, True), cross)
    param_anom = every_param - jnp.mean(every_param, axis=0)
    own_weights = lax.dynamic_slice_in_dim(
        weights, lax.axis_index("ens") * members_here, members_here, 1
    )
    new_params = (
        params + jnp.dot(own_weights.T, param_anom, precision=lax.Precision.HIGHEST) * norm_factor
    )
    return (new_states, new_params)


def solution(mesh):
    in_specs = (
        P("tm", "ens", "space", None),
        P("space", None),
        P("space", None),
        P("space", None),
        P("space", None),
        P("ens", None),
        P("tm", "space"),
        P("tm", "space"),
        P("tm", "space", None),
        P("tm", "space"),
    )
    out_specs = (P("tm", "ens", "space", None), P("ens", None))
    return jax.shard_map(
        per_device, mesh=mesh, in_specs=in_specs, out_specs=out_specs, check_vma=False
    )
```

```python
import math

import jax
import jax.numpy as jnp
from jax import lax
from jax.sharding import PartitionSpec as P

FINE = 4


FINE_DT = 0.25


def with_halo(cells, axis, width):
    count = lax.axis_size(axis)
    ends = count - 1
    head = cells[:, :width]
    tail = cells[:, cells.shape[1] - width :]
    return jnp.concatenate(
        [
            lax.ppermute(tail, axis, [(i, i + 1) for i in range(ends)]),
            cells,
            lax.ppermute(head, axis, [(i + 1, i) for i in range(ends)]),
        ],
        axis=1,
    )


def both_halves(value, axis):
    other = lax.ppermute(value, axis, [(0, 1), (1, 0)])
    first = lax.axis_index(axis) == 0
    return jnp.where(first, jnp.concatenate([value, other]), jnp.concatenate([other, value]))


def advance(values_in, coeffs, inside, step_size, forcing):
    middle = values_in[:, 1:-1, :]
    above_row = values_in[:, :-2, :]
    below_row = values_in[:, 2:, :]
    west_cell = jnp.pad(middle[:, :, :-1], ((0, 0), (0, 0), (1, 0)))
    east_cell = jnp.pad(middle[:, :, 1:], ((0, 0), (0, 0), (0, 1)))
    spread_term = coeffs[0] * (above_row + below_row + west_cell + east_cell - 4.0 * middle)
    tendency = (
        spread_term
        - coeffs[1] * (east_cell - west_cell) * 0.5
        - coeffs[2] * (below_row - above_row) * 0.5
    )
    if forcing is not None:
        tendency = tendency + forcing
    return (middle + step_size * tendency) * inside


def per_device(
    start_states,
    velocity_x,
    velocity_y,
    diffusivity,
    source_shape,
    params,
    obs_cell,
    obs_data,
    obs_noise,
    obs_var,
):
    coarse_dt = FINE_DT * FINE
    state = start_states[0]
    members_here, row_count, col_count = state.shape
    slabs = row_count * lax.axis_size("space")
    first_row = lax.axis_index("space") * row_count
    slice_index = lax.axis_index("tm")
    slices = lax.axis_size("tm")
    links = slices - 1
    depth = FINE + links
    group = members_here // slices
    band_width = col_count // params.shape[1]

    mine = lax.all_to_all(
        state.reshape(slices, group, row_count, col_count), "tm", 0, 0, tiled=True
    ).reshape(slices * group, row_count, col_count)
    my_params = lax.dynamic_slice_in_dim(params, slice_index * group, group, 0)
    spread_params = jnp.repeat(my_params, band_width, axis=1)

    fields = jnp.stack([diffusivity, velocity_x, velocity_y, source_shape])
    wide = with_halo(jnp.concatenate([mine, fields]), "space", depth)
    count = slices * group
    wide_state = wide[:count]
    wide_coeffs = wide[count : count + 3]
    wide_forcing = jnp.tile(wide[count + 3][None] * spread_params[:, None, :], (slices, 1, 1))
    global_rows = first_row - depth + jnp.arange(row_count + 2 * depth, dtype=jnp.int32)
    wide_inside = ((global_rows >= 0) & (global_rows < slabs)).astype(jnp.float32)[:, None]

    def step(values, low, step_size, forcing):
        n = values.shape[1]
        lo, hi = low + 1, low + n - 1
        q = None if forcing is None else forcing[:, lo:hi]
        return advance(values, wide_coeffs[:, lo:hi], wide_inside[lo:hi], step_size, q)

    current = wide_state
    coarse_part = step(wide_state, 0, coarse_dt, None)
    for section in range(FINE):
        current = step(current, section, FINE_DT, wide_forcing)
    coarse_part = coarse_part[:, FINE - 1 : FINE - 1 + current.shape[1]]
    fine = current.reshape(slices, group, -1, col_count)
    coarse_part = coarse_part.reshape(slices, group, -1, col_count)
    running = fine[0]
    results = [running[:, links : links + row_count]]
    for link in range(1, slices):
        correction = fine[link] - coarse_part[link]
        stepped = step(running, FINE + link - 1, coarse_dt, None)
        running = correction[:, link : correction.shape[1] - link] + stepped
        results.append(running[:, links - link : links - link + row_count])
    done = jnp.stack(results)
    running = lax.all_to_all(done, "tm", 0, 0, tiled=True).reshape(
        members_here, row_count, col_count
    )
    new_states = running[None]

    every_cell = lax.all_gather(obs_cell[0], "tm")
    local_cell = every_cell - first_row * col_count
    rows = local_cell // col_count
    cols = local_cell % col_count
    picked_rows = jnp.take_along_axis(done, rows[:, None, :, None], axis=2)
    at_col = lax.broadcasted_iota(jnp.int32, picked_rows.shape, 3) == cols[:, None, :, None]
    local_pred = jnp.sum(jnp.where(at_col, picked_rows, 0.0), axis=3)

    obs_here = obs_cell.shape[1]
    pieces = [local_pred.reshape(-1), obs_data[0], obs_var[0], obs_noise[0].reshape(-1)]
    used = sum(piece.size for piece in pieces)
    width = max(2048, used)
    shard = jnp.concatenate(pieces + [jnp.zeros((width - used,), jnp.float32)])
    spaces = lax.axis_size("space")
    halves = lax.axis_size("ens")
    gathered = lax.all_gather(shard, ("tm", "space", "ens")).reshape(slices, spaces, halves, width)
    total = members_here * halves
    cut = slices * group * obs_here
    pred = gathered[..., :cut].reshape(slices, spaces, halves, slices, group, obs_here)
    every_pred = jnp.transpose(pred, (2, 0, 4, 3, 1, 5)).reshape(total, -1)
    at_obs = gathered[:, :, 0, cut:]
    every_data = at_obs[..., :obs_here].reshape(-1)
    every_var = at_obs[..., obs_here : 2 * obs_here].reshape(-1)
    noise = at_obs[..., 2 * obs_here : 2 * obs_here + obs_here * total]
    noise = jnp.transpose(noise.reshape(slices, spaces, obs_here, total), (3, 0, 1, 2))
    noise = noise.reshape(total, -1)
    every_param = both_halves(params, "ens")
    norm_factor = 1.0 / math.sqrt(total - 1)
    inv_spread = lax.rsqrt(every_var)[None, :]
    pred_mean = jnp.mean(every_pred, axis=0, keepdims=True)
    anomaly = (every_pred - pred_mean) * (inv_spread * norm_factor)
    misfit = (every_data[None, :] + noise - every_pred) * inv_spread
    gram = jnp.dot(anomaly, anomaly.T, precision=lax.Precision.HIGHEST)
    cross = jnp.dot(anomaly, misfit.T, precision=lax.Precision.HIGHEST)
    system = jnp.eye(total, dtype=jnp.float32) + gram
    factor = jnp.linalg.cholesky(system)
    weights = jax.scipy.linalg.cho_solve((factor, True), cross)
    param_anom = every_param - jnp.mean(every_param, axis=0)
    own_weights = lax.dynamic_slice_in_dim(
        weights, lax.axis_index("ens") * members_here, members_here, 1
    )
    new_params = (
        params + jnp.dot(own_weights.T, param_anom, precision=lax.Precision.HIGHEST) * norm_factor
    )
    return (new_states, new_params)


def solution(mesh):
    in_specs = (
        P("tm", "ens", "space", None),
        P("space", None),
        P("space", None),
        P("space", None),
        P("space", None),
        P("ens", None),
        P("tm", "space"),
        P("tm", "space"),
        P("tm", "space", None),
        P("tm", "space"),
    )
    out_specs = (P("tm", "ens", "space", None), P("ens", None))
    return jax.shard_map(
        per_device, mesh=mesh, in_specs=in_specs, out_specs=out_specs, check_vma=False
    )
```

```python
import math

import jax
import jax.numpy as jnp
from jax import lax
from jax.sharding import PartitionSpec as P

FINE = 4


FINE_DT = 0.25


def with_halo(cells, axis, width):
    count = lax.axis_size(axis)
    ends = count - 1
    head = cells[:, :width]
    tail = cells[:, cells.shape[1] - width :]
    return jnp.concatenate(
        [
            lax.ppermute(tail, axis, [(i, i + 1) for i in range(ends)]),
            cells,
            lax.ppermute(head, axis, [(i + 1, i) for i in range(ends)]),
        ],
        axis=1,
    )


def butterfly_sum(value, axis):
    count = lax.axis_size(axis)
    if count & (count - 1):
        return lax.psum(value, axis)
    bit = 1
    while bit < count:
        value = value + lax.ppermute(value, axis, [(i, i ^ bit) for i in range(count)])
        bit *= 2
    return value


def by_source(pieces, axis):
    count = lax.axis_size(axis)
    mirrored = [pieces[(-j) % count] for j in range(count)]
    doubled = jnp.stack(mirrored + mirrored)
    start = (count - lax.axis_index(axis)) % count
    return lax.dynamic_slice_in_dim(doubled, start, count, 0)


def shift(value, axis, d):
    count = lax.axis_size(axis)
    return lax.ppermute(value, axis, [(i, (i + d) % count) for i in range(count)])


def gather_axis(value, axis):
    count = lax.axis_size(axis)
    return by_source([value] + [shift(value, axis, d) for d in range(1, count)], axis)


def exchange_axis(values, axis):
    count = lax.axis_size(axis)
    own = lax.axis_index(axis)
    pieces = [jnp.take(values, own, axis=0)] + [
        shift(jnp.take(values, (own + d) % count, axis=0), axis, d) for d in range(1, count)
    ]
    return by_source(pieces, axis)


def both_halves(value, axis):
    other = lax.ppermute(value, axis, [(0, 1), (1, 0)])
    first = lax.axis_index(axis) == 0
    return jnp.where(first, jnp.concatenate([value, other]), jnp.concatenate([other, value]))


def advance(values_in, coeffs, inside, step_size, forcing):
    middle = values_in[:, 1:-1, :]
    above_row = values_in[:, :-2, :]
    below_row = values_in[:, 2:, :]
    west_cell = jnp.pad(middle[:, :, :-1], ((0, 0), (0, 0), (1, 0)))
    east_cell = jnp.pad(middle[:, :, 1:], ((0, 0), (0, 0), (0, 1)))
    spread_term = coeffs[0] * (above_row + below_row + west_cell + east_cell - 4.0 * middle)
    tendency = (
        spread_term
        - coeffs[1] * (east_cell - west_cell) * 0.5
        - coeffs[2] * (below_row - above_row) * 0.5
    )
    if forcing is not None:
        tendency = tendency + forcing
    return (middle + step_size * tendency) * inside


def per_device(
    start_states,
    velocity_x,
    velocity_y,
    diffusivity,
    source_shape,
    params,
    obs_cell,
    obs_data,
    obs_noise,
    obs_var,
):
    coarse_dt = FINE_DT * FINE
    state = start_states[0]
    members_here, row_count, col_count = state.shape
    slabs = row_count * lax.axis_size("space")
    first_row = lax.axis_index("space") * row_count
    slice_index = lax.axis_index("tm")
    slices = lax.axis_size("tm")
    links = slices - 1
    depth = FINE + links
    group = members_here // slices
    band_width = col_count // params.shape[1]

    mine = lax.all_to_all(
        state.reshape(slices, group, row_count, col_count), "tm", 0, 0, tiled=True
    ).reshape(slices * group, row_count, col_count)
    my_params = lax.dynamic_slice_in_dim(params, slice_index * group, group, 0)
    spread_params = jnp.repeat(my_params, band_width, axis=1)

    fields = jnp.stack([diffusivity, velocity_x, velocity_y, source_shape])
    wide = with_halo(jnp.concatenate([mine, fields]), "space", depth)
    count = slices * group
    wide_state = wide[:count]
    wide_coeffs = wide[count : count + 3]
    wide_forcing = jnp.tile(wide[count + 3][None] * spread_params[:, None, :], (slices, 1, 1))
    global_rows = first_row - depth + jnp.arange(row_count + 2 * depth, dtype=jnp.int32)
    wide_inside = ((global_rows >= 0) & (global_rows < slabs)).astype(jnp.float32)[:, None]

    def step(values, low, step_size, forcing):
        n = values.shape[1]
        lo, hi = low + 1, low + n - 1
        q = None if forcing is None else forcing[:, lo:hi]
        return advance(values, wide_coeffs[:, lo:hi], wide_inside[lo:hi], step_size, q)

    current = wide_state
    coarse_part = step(wide_state, 0, coarse_dt, None)
    for section in range(FINE):
        current = step(current, section, FINE_DT, wide_forcing)
    coarse_part = coarse_part[:, FINE - 1 : FINE - 1 + current.shape[1]]
    fine = current.reshape(slices, group, -1, col_count)
    coarse_part = coarse_part.reshape(slices, group, -1, col_count)
    running = fine[0]
    results = [running[:, links : links + row_count]]
    for link in range(1, slices):
        correction = fine[link] - coarse_part[link]
        stepped = step(running, FINE + link - 1, coarse_dt, None)
        running = correction[:, link : correction.shape[1] - link] + stepped
        results.append(running[:, links - link : links - link + row_count])
    done = jnp.stack(results)
    running = exchange_axis(done, "tm").reshape(members_here, row_count, col_count)
    new_states = running[None]

    obs_pack = jnp.concatenate(
        [
            obs_cell[0].astype(jnp.float32)[:, None],
            obs_data[0][:, None],
            obs_var[0][:, None],
            obs_noise[0],
        ],
        axis=1,
    )
    every_obs = gather_axis(obs_pack, "tm")
    every_cell = every_obs[:, :, 0].astype(jnp.int32)
    every_data = every_obs[:, :, 1]
    every_var = every_obs[:, :, 2]
    every_noise = every_obs[:, :, 3:]

    local_cell = every_cell - first_row * col_count
    rows = local_cell // col_count
    cols = local_cell % col_count
    picked_rows = jnp.take_along_axis(done, rows[:, None, :, None], axis=2)
    at_col = lax.broadcasted_iota(jnp.int32, picked_rows.shape, 3) == cols[:, None, :, None]
    local_pred = jnp.sum(jnp.where(at_col, picked_rows, 0.0), axis=3)
    pred = gather_axis(local_pred, "tm")
    pred = jnp.transpose(pred, (0, 2, 1, 3)).reshape(members_here, -1)
    every_pred = both_halves(pred, "ens")
    every_param = both_halves(params, "ens")
    total = every_pred.shape[0]
    norm_factor = 1.0 / math.sqrt(total - 1)
    inv_spread = lax.rsqrt(every_var).reshape(1, -1)
    pred_mean = jnp.mean(every_pred, axis=0, keepdims=True)
    anomaly = (every_pred - pred_mean) * (inv_spread * norm_factor)
    noise = jnp.transpose(every_noise, (2, 0, 1)).reshape(total, -1)
    misfit = (every_data.reshape(1, -1) + noise - every_pred) * inv_spread
    gram = jnp.dot(anomaly, anomaly.T, precision=lax.Precision.HIGHEST)
    cross = jnp.dot(anomaly, misfit.T, precision=lax.Precision.HIGHEST)
    sums = butterfly_sum(jnp.stack([gram, cross]), "space")
    gram, cross = sums[0], sums[1]
    system = jnp.eye(total, dtype=jnp.float32) + gram
    factor = jnp.linalg.cholesky(system)
    weights = jax.scipy.linalg.cho_solve((factor, True), cross)
    param_anom = every_param - jnp.mean(every_param, axis=0)
    own_weights = lax.dynamic_slice_in_dim(
        weights, lax.axis_index("ens") * members_here, members_here, 1
    )
    new_params = (
        params + jnp.dot(own_weights.T, param_anom, precision=lax.Precision.HIGHEST) * norm_factor
    )
    return (new_states, new_params)


def solution(mesh):
    in_specs = (
        P("tm", "ens", "space", None),
        P("space", None),
        P("space", None),
        P("space", None),
        P("space", None),
        P("ens", None),
        P("tm", "space"),
        P("tm", "space"),
        P("tm", "space", None),
        P("tm", "space"),
    )
    out_specs = (P("tm", "ens", "space", None), P("ens", None))
    return jax.shard_map(
        per_device, mesh=mesh, in_specs=in_specs, out_specs=out_specs, check_vma=False
    )
```

```python
import math

import jax
import jax.numpy as jnp
from jax import lax
from jax.sharding import PartitionSpec as P

FINE = 4


FINE_DT = 0.25


def with_halo(cells, axis, width):
    count = lax.axis_size(axis)
    ends = count - 1
    head = cells[:, :width]
    tail = cells[:, cells.shape[1] - width :]
    return jnp.concatenate(
        [
            lax.ppermute(tail, axis, [(i, i + 1) for i in range(ends)]),
            cells,
            lax.ppermute(head, axis, [(i + 1, i) for i in range(ends)]),
        ],
        axis=1,
    )


def butterfly_sum(value, axis):
    count = lax.axis_size(axis)
    if count & (count - 1):
        return lax.psum(value, axis)
    bit = 1
    while bit < count:
        value = value + lax.ppermute(value, axis, [(i, i ^ bit) for i in range(count)])
        bit *= 2
    return value


def both_halves(value, axis):
    other = lax.ppermute(value, axis, [(0, 1), (1, 0)])
    first = lax.axis_index(axis) == 0
    return jnp.where(first, jnp.concatenate([value, other]), jnp.concatenate([other, value]))


def advance(values_in, coeffs, inside, step_size, forcing):
    middle = values_in[:, 1:-1, :]
    above_row = values_in[:, :-2, :]
    below_row = values_in[:, 2:, :]
    west_cell = jnp.pad(middle[:, :, :-1], ((0, 0), (0, 0), (1, 0)))
    east_cell = jnp.pad(middle[:, :, 1:], ((0, 0), (0, 0), (0, 1)))
    spread_term = coeffs[0] * (above_row + below_row + west_cell + east_cell - 4.0 * middle)
    tendency = (
        spread_term
        - coeffs[1] * (east_cell - west_cell) * 0.5
        - coeffs[2] * (below_row - above_row) * 0.5
    )
    if forcing is not None:
        tendency = tendency + forcing
    return (middle + step_size * tendency) * inside


def per_device(
    start_states,
    velocity_x,
    velocity_y,
    diffusivity,
    source_shape,
    params,
    obs_cell,
    obs_data,
    obs_noise,
    obs_var,
):
    coarse_dt = FINE_DT * FINE
    state = start_states[0]
    members_here, row_count, col_count = state.shape
    slabs = row_count * lax.axis_size("space")
    first_row = lax.axis_index("space") * row_count
    slice_index = lax.axis_index("tm")
    slices = lax.axis_size("tm")
    links = slices - 1
    depth = FINE + links
    group = members_here // slices
    band_width = col_count // params.shape[1]

    mine = lax.all_to_all(
        state.reshape(slices, group, row_count, col_count), "tm", 0, 0, tiled=True
    ).reshape(slices * group, row_count, col_count)
    my_params = lax.dynamic_slice_in_dim(params, slice_index * group, group, 0)
    spread_params = jnp.repeat(my_params, band_width, axis=1)

    fields = jnp.stack([diffusivity, velocity_x, velocity_y, source_shape])
    wide = with_halo(jnp.concatenate([mine, fields]), "space", depth)
    count = slices * group
    wide_state = wide[:count]
    wide_coeffs = wide[count : count + 3]
    wide_forcing = jnp.tile(wide[count + 3][None] * spread_params[:, None, :], (slices, 1, 1))
    global_rows = first_row - depth + jnp.arange(row_count + 2 * depth, dtype=jnp.int32)
    wide_inside = ((global_rows >= 0) & (global_rows < slabs)).astype(jnp.float32)[:, None]

    def step(values, low, step_size, forcing):
        n = values.shape[1]
        lo, hi = low + 1, low + n - 1
        q = None if forcing is None else forcing[:, lo:hi]
        return advance(values, wide_coeffs[:, lo:hi], wide_inside[lo:hi], step_size, q)

    current = wide_state
    coarse_part = step(wide_state, 0, coarse_dt, None)
    for section in range(FINE):
        current = step(current, section, FINE_DT, wide_forcing)
    coarse_part = coarse_part[:, FINE - 1 : FINE - 1 + current.shape[1]]
    fine = current.reshape(slices, group, -1, col_count)
    coarse_part = coarse_part.reshape(slices, group, -1, col_count)
    running = fine[0]
    results = [running[:, links : links + row_count]]
    for link in range(1, slices):
        correction = fine[link] - coarse_part[link]
        stepped = step(running, FINE + link - 1, coarse_dt, None)
        running = correction[:, link : correction.shape[1] - link] + stepped
        results.append(running[:, links - link : links - link + row_count])
    done = jnp.stack(results)
    running = lax.all_to_all(done, "tm", 0, 0, tiled=True).reshape(
        members_here, row_count, col_count
    )
    new_states = running[None]

    local_cell = obs_cell[0] - first_row * col_count
    rows = local_cell // col_count
    cols = local_cell % col_count
    row_pick = (rows[:, None] == jnp.arange(row_count, dtype=jnp.int32)[None, :]).astype(jnp.float32)
    picked_rows = jnp.einsum("or,mrc->moc", row_pick, running, precision=lax.Precision.HIGHEST)
    at_col = lax.broadcasted_iota(jnp.int32, picked_rows.shape, 2) == cols[None, :, None]
    predicted = jnp.sum(jnp.where(at_col, picked_rows, 0.0), axis=2)
    every_pred = both_halves(predicted, "ens")
    every_param = both_halves(params, "ens")
    total = every_pred.shape[0]
    norm_factor = 1.0 / math.sqrt(total - 1)
    inv_spread = lax.rsqrt(obs_var[0])[None, :]
    pred_mean = jnp.mean(every_pred, axis=0, keepdims=True)
    anomaly = (every_pred - pred_mean) * (inv_spread * norm_factor)
    misfit = (obs_data[0][None, :] + obs_noise[0].T - every_pred) * inv_spread
    gram = jnp.dot(anomaly, anomaly.T, precision=lax.Precision.HIGHEST)
    cross = jnp.dot(anomaly, misfit.T, precision=lax.Precision.HIGHEST)
    sums = jnp.stack([gram, cross])
    sums = butterfly_sum(sums, "tm")
    sums = butterfly_sum(sums, "space")
    gram, cross = sums[0], sums[1]
    system = jnp.eye(total, dtype=jnp.float32) + gram
    factor = jnp.linalg.cholesky(system)
    weights = jax.scipy.linalg.cho_solve((factor, True), cross)
    param_anom = every_param - jnp.mean(every_param, axis=0)
    own_weights = lax.dynamic_slice_in_dim(
        weights, lax.axis_index("ens") * members_here, members_here, 1
    )
    new_params = (
        params + jnp.dot(own_weights.T, param_anom, precision=lax.Precision.HIGHEST) * norm_factor
    )
    return (new_states, new_params)


def solution(mesh):
    in_specs = (
        P("tm", "ens", "space", None),
        P("space", None),
        P("space", None),
        P("space", None),
        P("space", None),
        P("ens", None),
        P("tm", "space"),
        P("tm", "space"),
        P("tm", "space", None),
        P("tm", "space"),
    )
    out_specs = (P("tm", "ens", "space", None), P("ens", None))
    return jax.shard_map(
        per_device, mesh=mesh, in_specs=in_specs, out_specs=out_specs, check_vma=False
    )
```

```python
import math

import jax
import jax.numpy as jnp
from jax import lax
from jax.sharding import PartitionSpec as P

FINE = 4


FINE_DT = 0.25


def with_halo(cells, axis, width):
    count = lax.axis_size(axis)
    ends = count - 1
    head = cells[:, :width]
    tail = cells[:, cells.shape[1] - width :]
    return jnp.concatenate(
        [
            lax.ppermute(tail, axis, [(i, i + 1) for i in range(ends)]),
            cells,
            lax.ppermute(head, axis, [(i + 1, i) for i in range(ends)]),
        ],
        axis=1,
    )


def quad_sum(value, axis):
    count = lax.axis_size(axis)
    if count & (count - 1):
        return lax.psum(value, axis)
    bit = 1
    while bit < count:
        if bit * 4 <= count:
            near, far, both = (
                lax.ppermute(value, axis, [(i, i ^ (k * bit)) for i in range(count)])
                for k in (1, 2, 3)
            )
            value = (value + near) + (far + both)
            bit *= 4
        else:
            value = value + lax.ppermute(value, axis, [(i, i ^ bit) for i in range(count)])
            bit *= 2
    return value


def both_halves(value, axis):
    other = lax.ppermute(value, axis, [(0, 1), (1, 0)])
    first = lax.axis_index(axis) == 0
    return jnp.where(first, jnp.concatenate([value, other]), jnp.concatenate([other, value]))


def advance(values_in, coeffs, inside, step_size, forcing):
    middle = values_in[:, 1:-1, :]
    above_row = values_in[:, :-2, :]
    below_row = values_in[:, 2:, :]
    west_cell = jnp.pad(middle[:, :, :-1], ((0, 0), (0, 0), (1, 0)))
    east_cell = jnp.pad(middle[:, :, 1:], ((0, 0), (0, 0), (0, 1)))
    spread_term = coeffs[0] * (above_row + below_row + west_cell + east_cell - 4.0 * middle)
    tendency = (
        spread_term
        - coeffs[1] * (east_cell - west_cell) * 0.5
        - coeffs[2] * (below_row - above_row) * 0.5
    )
    if forcing is not None:
        tendency = tendency + forcing
    return (middle + step_size * tendency) * inside


def per_device(
    start_states,
    velocity_x,
    velocity_y,
    diffusivity,
    source_shape,
    params,
    obs_cell,
    obs_data,
    obs_noise,
    obs_var,
):
    coarse_dt = FINE_DT * FINE
    state = start_states[0]
    members_here, row_count, col_count = state.shape
    slabs = row_count * lax.axis_size("space")
    first_row = lax.axis_index("space") * row_count
    slice_index = lax.axis_index("tm")
    slices = lax.axis_size("tm")
    links = slices - 1
    depth = FINE + links
    group = members_here // slices
    band_width = col_count // params.shape[1]

    mine = lax.all_to_all(
        state.reshape(slices, group, row_count, col_count), "tm", 0, 0, tiled=True
    ).reshape(slices * group, row_count, col_count)
    my_params = lax.dynamic_slice_in_dim(params, slice_index * group, group, 0)
    spread_params = jnp.repeat(my_params, band_width, axis=1)

    fields = jnp.stack([diffusivity, velocity_x, velocity_y, source_shape])
    wide = with_halo(jnp.concatenate([mine, fields]), "space", depth)
    count = slices * group
    wide_state = wide[:count]
    wide_coeffs = wide[count : count + 3]
    wide_forcing = jnp.tile(wide[count + 3][None] * spread_params[:, None, :], (slices, 1, 1))
    global_rows = first_row - depth + jnp.arange(row_count + 2 * depth, dtype=jnp.int32)
    wide_inside = ((global_rows >= 0) & (global_rows < slabs)).astype(jnp.float32)[:, None]

    def step(values, low, step_size, forcing):
        n = values.shape[1]
        lo, hi = low + 1, low + n - 1
        q = None if forcing is None else forcing[:, lo:hi]
        return advance(values, wide_coeffs[:, lo:hi], wide_inside[lo:hi], step_size, q)

    current = wide_state
    coarse_part = step(wide_state, 0, coarse_dt, None)
    for section in range(FINE):
        current = step(current, section, FINE_DT, wide_forcing)
    coarse_part = coarse_part[:, FINE - 1 : FINE - 1 + current.shape[1]]
    fine = current.reshape(slices, group, -1, col_count)
    coarse_part = coarse_part.reshape(slices, group, -1, col_count)
    running = fine[0]
    results = [running[:, links : links + row_count]]
    for link in range(1, slices):
        correction = fine[link] - coarse_part[link]
        stepped = step(running, FINE + link - 1, coarse_dt, None)
        running = correction[:, link : correction.shape[1] - link] + stepped
        results.append(running[:, links - link : links - link + row_count])
    done = jnp.stack(results)
    running = lax.all_to_all(done, "tm", 0, 0, tiled=True).reshape(
        members_here, row_count, col_count
    )
    new_states = running[None]

    local_cell = obs_cell[0] - first_row * col_count
    rows = local_cell // col_count
    cols = local_cell % col_count
    row_pick = (rows[:, None] == jnp.arange(row_count, dtype=jnp.int32)[None, :]).astype(jnp.float32)
    picked_rows = jnp.einsum("or,mrc->moc", row_pick, running, precision=lax.Precision.HIGHEST)
    at_col = lax.broadcasted_iota(jnp.int32, picked_rows.shape, 2) == cols[None, :, None]
    predicted = jnp.sum(jnp.where(at_col, picked_rows, 0.0), axis=2)
    every_pred = both_halves(predicted, "ens")
    every_param = both_halves(params, "ens")
    total = every_pred.shape[0]
    norm_factor = 1.0 / math.sqrt(total - 1)
    inv_spread = lax.rsqrt(obs_var[0])[None, :]
    pred_mean = jnp.mean(every_pred, axis=0, keepdims=True)
    anomaly = (every_pred - pred_mean) * (inv_spread * norm_factor)
    misfit = (obs_data[0][None, :] + obs_noise[0].T - every_pred) * inv_spread
    gram = jnp.dot(anomaly, anomaly.T, precision=lax.Precision.HIGHEST)
    cross = jnp.dot(anomaly, misfit.T, precision=lax.Precision.HIGHEST)
    sums = jnp.stack([gram, cross])
    sums = quad_sum(sums, "tm")
    sums = quad_sum(sums, "space")
    gram, cross = sums[0], sums[1]
    system = jnp.eye(total, dtype=jnp.float32) + gram
    factor = jnp.linalg.cholesky(system)
    weights = jax.scipy.linalg.cho_solve((factor, True), cross)
    param_anom = every_param - jnp.mean(every_param, axis=0)
    own_weights = lax.dynamic_slice_in_dim(
        weights, lax.axis_index("ens") * members_here, members_here, 1
    )
    new_params = (
        params + jnp.dot(own_weights.T, param_anom, precision=lax.Precision.HIGHEST) * norm_factor
    )
    return (new_states, new_params)


def solution(mesh):
    in_specs = (
        P("tm", "ens", "space", None),
        P("space", None),
        P("space", None),
        P("space", None),
        P("space", None),
        P("ens", None),
        P("tm", "space"),
        P("tm", "space"),
        P("tm", "space", None),
        P("tm", "space"),
    )
    out_specs = (P("tm", "ens", "space", None), P("ens", None))
    return jax.shard_map(
        per_device, mesh=mesh, in_specs=in_specs, out_specs=out_specs, check_vma=False
    )
```

```python
import math

import jax
import jax.numpy as jnp
from jax import lax
from jax.sharding import PartitionSpec as P

FINE = 4


FINE_DT = 0.25


def with_halo(cells, axis, width):
    count = lax.axis_size(axis)
    ends = count - 1
    head = cells[:, :width]
    tail = cells[:, cells.shape[1] - width :]
    return jnp.concatenate(
        [
            lax.ppermute(tail, axis, [(i, i + 1) for i in range(ends)]),
            cells,
            lax.ppermute(head, axis, [(i + 1, i) for i in range(ends)]),
        ],
        axis=1,
    )


def group_sum(value, axis, radix):
    count = lax.axis_size(axis)
    if count & (count - 1):
        return lax.psum(value, axis)
    bit = 1
    while bit < count:
        width = min(radix, count // bit)
        parts = [value] + [
            lax.ppermute(value, axis, [(i, i ^ (k * bit)) for i in range(count)])
            for k in range(1, width)
        ]
        while len(parts) > 1:
            parts = [parts[j] + parts[j + 1] for j in range(0, len(parts), 2)]
        value = parts[0]
        bit *= width
    return value


def both_halves(value, axis):
    other = lax.ppermute(value, axis, [(0, 1), (1, 0)])
    first = lax.axis_index(axis) == 0
    return jnp.where(first, jnp.concatenate([value, other]), jnp.concatenate([other, value]))


def advance(values_in, coeffs, inside, step_size, forcing):
    middle = values_in[:, 1:-1, :]
    above_row = values_in[:, :-2, :]
    below_row = values_in[:, 2:, :]
    west_cell = jnp.pad(middle[:, :, :-1], ((0, 0), (0, 0), (1, 0)))
    east_cell = jnp.pad(middle[:, :, 1:], ((0, 0), (0, 0), (0, 1)))
    spread_term = coeffs[0] * (above_row + below_row + west_cell + east_cell - 4.0 * middle)
    tendency = (
        spread_term
        - coeffs[1] * (east_cell - west_cell) * 0.5
        - coeffs[2] * (below_row - above_row) * 0.5
    )
    if forcing is not None:
        tendency = tendency + forcing
    return (middle + step_size * tendency) * inside


def per_device(
    start_states,
    velocity_x,
    velocity_y,
    diffusivity,
    source_shape,
    params,
    obs_cell,
    obs_data,
    obs_noise,
    obs_var,
):
    coarse_dt = FINE_DT * FINE
    state = start_states[0]
    members_here, row_count, col_count = state.shape
    slabs = row_count * lax.axis_size("space")
    first_row = lax.axis_index("space") * row_count
    slice_index = lax.axis_index("tm")
    slices = lax.axis_size("tm")
    links = slices - 1
    depth = FINE + links
    group = members_here // slices
    band_width = col_count // params.shape[1]

    mine = lax.all_to_all(
        state.reshape(slices, group, row_count, col_count), "tm", 0, 0, tiled=True
    ).reshape(slices * group, row_count, col_count)
    my_params = lax.dynamic_slice_in_dim(params, slice_index * group, group, 0)
    spread_params = jnp.repeat(my_params, band_width, axis=1)

    fields = jnp.stack([diffusivity, velocity_x, velocity_y, source_shape])
    wide = with_halo(jnp.concatenate([mine, fields]), "space", depth)
    count = slices * group
    wide_state = wide[:count]
    wide_coeffs = wide[count : count + 3]
    wide_forcing = jnp.tile(wide[count + 3][None] * spread_params[:, None, :], (slices, 1, 1))
    global_rows = first_row - depth + jnp.arange(row_count + 2 * depth, dtype=jnp.int32)
    wide_inside = ((global_rows >= 0) & (global_rows < slabs)).astype(jnp.float32)[:, None]

    def step(values, low, step_size, forcing):
        n = values.shape[1]
        lo, hi = low + 1, low + n - 1
        q = None if forcing is None else forcing[:, lo:hi]
        return advance(values, wide_coeffs[:, lo:hi], wide_inside[lo:hi], step_size, q)

    current = wide_state
    coarse_part = step(wide_state, 0, coarse_dt, None)
    for section in range(FINE):
        current = step(current, section, FINE_DT, wide_forcing)
    coarse_part = coarse_part[:, FINE - 1 : FINE - 1 + current.shape[1]]
    fine = current.reshape(slices, group, -1, col_count)
    coarse_part = coarse_part.reshape(slices, group, -1, col_count)
    running = fine[0]
    results = [running[:, links : links + row_count]]
    for link in range(1, slices):
        correction = fine[link] - coarse_part[link]
        stepped = step(running, FINE + link - 1, coarse_dt, None)
        running = correction[:, link : correction.shape[1] - link] + stepped
        results.append(running[:, links - link : links - link + row_count])
    done = jnp.stack(results)
    running = lax.all_to_all(done, "tm", 0, 0, tiled=True).reshape(
        members_here, row_count, col_count
    )
    new_states = running[None]

    local_cell = obs_cell[0] - first_row * col_count
    rows = local_cell // col_count
    cols = local_cell % col_count
    row_pick = (rows[:, None] == jnp.arange(row_count, dtype=jnp.int32)[None, :]).astype(jnp.float32)
    picked_rows = jnp.einsum("or,mrc->moc", row_pick, running, precision=lax.Precision.HIGHEST)
    at_col = lax.broadcasted_iota(jnp.int32, picked_rows.shape, 2) == cols[None, :, None]
    predicted = jnp.sum(jnp.where(at_col, picked_rows, 0.0), axis=2)
    every_pred = both_halves(predicted, "ens")
    every_param = both_halves(params, "ens")
    total = every_pred.shape[0]
    norm_factor = 1.0 / math.sqrt(total - 1)
    inv_spread = lax.rsqrt(obs_var[0])[None, :]
    pred_mean = jnp.mean(every_pred, axis=0, keepdims=True)
    anomaly = (every_pred - pred_mean) * (inv_spread * norm_factor)
    misfit = (obs_data[0][None, :] + obs_noise[0].T - every_pred) * inv_spread
    gram = jnp.dot(anomaly, anomaly.T, precision=lax.Precision.HIGHEST)
    cross = jnp.dot(anomaly, misfit.T, precision=lax.Precision.HIGHEST)
    sums = jnp.stack([gram, cross])
    sums = group_sum(sums, "tm", 4)
    sums = group_sum(sums, "space", 16)
    gram, cross = sums[0], sums[1]
    system = jnp.eye(total, dtype=jnp.float32) + gram
    factor = jnp.linalg.cholesky(system)
    weights = jax.scipy.linalg.cho_solve((factor, True), cross)
    param_anom = every_param - jnp.mean(every_param, axis=0)
    own_weights = lax.dynamic_slice_in_dim(
        weights, lax.axis_index("ens") * members_here, members_here, 1
    )
    new_params = (
        params + jnp.dot(own_weights.T, param_anom, precision=lax.Precision.HIGHEST) * norm_factor
    )
    return (new_states, new_params)


def solution(mesh):
    in_specs = (
        P("tm", "ens", "space", None),
        P("space", None),
        P("space", None),
        P("space", None),
        P("space", None),
        P("ens", None),
        P("tm", "space"),
        P("tm", "space"),
        P("tm", "space", None),
        P("tm", "space"),
    )
    out_specs = (P("tm", "ens", "space", None), P("ens", None))
    return jax.shard_map(
        per_device, mesh=mesh, in_specs=in_specs, out_specs=out_specs, check_vma=False
    )
```

```python
import math

import jax
import jax.numpy as jnp
from jax import lax
from jax.sharding import PartitionSpec as P

FINE = 4


FINE_DT = 0.25


def with_halo(cells, axis, width):
    count = lax.axis_size(axis)
    ends = count - 1
    head = cells[:, :width]
    tail = cells[:, cells.shape[1] - width :]
    return jnp.concatenate(
        [
            lax.ppermute(tail, axis, [(i, i + 1) for i in range(ends)]),
            cells,
            lax.ppermute(head, axis, [(i + 1, i) for i in range(ends)]),
        ],
        axis=1,
    )


def quad_sum(value, axis):
    count = lax.axis_size(axis)
    if count & (count - 1):
        return lax.psum(value, axis)
    bit = 1
    while bit < count:
        if bit * 4 <= count:
            near, far, both = (
                lax.ppermute(value, axis, [(i, i ^ (k * bit)) for i in range(count)])
                for k in (1, 2, 3)
            )
            value = (value + near) + (far + both)
            bit *= 4
        else:
            value = value + lax.ppermute(value, axis, [(i, i ^ bit) for i in range(count)])
            bit *= 2
    return value


def both_halves(value, axis):
    other = lax.ppermute(value, axis, [(0, 1), (1, 0)])
    first = lax.axis_index(axis) == 0
    return jnp.where(first, jnp.concatenate([value, other]), jnp.concatenate([other, value]))


def advance(values_in, coeffs, inside, step_size, forcing):
    middle = values_in[:, 1:-1, :]
    above_row = values_in[:, :-2, :]
    below_row = values_in[:, 2:, :]
    west_cell = jnp.pad(middle[:, :, :-1], ((0, 0), (0, 0), (1, 0)))
    east_cell = jnp.pad(middle[:, :, 1:], ((0, 0), (0, 0), (0, 1)))
    spread_term = coeffs[0] * (above_row + below_row + west_cell + east_cell - 4.0 * middle)
    tendency = (
        spread_term
        - coeffs[1] * (east_cell - west_cell) * 0.5
        - coeffs[2] * (below_row - above_row) * 0.5
    )
    if forcing is not None:
        tendency = tendency + forcing
    return (middle + step_size * tendency) * inside


def per_device(
    start_states,
    velocity_x,
    velocity_y,
    diffusivity,
    source_shape,
    params,
    obs_cell,
    obs_data,
    obs_noise,
    obs_var,
):
    coarse_dt = FINE_DT * FINE
    state = start_states[0]
    members_here, row_count, col_count = state.shape
    slabs = row_count * lax.axis_size("space")
    first_row = lax.axis_index("space") * row_count
    slice_index = lax.axis_index("tm")
    slices = lax.axis_size("tm")
    links = slices - 1
    depth = FINE + links
    group = members_here // slices
    band_width = col_count // params.shape[1]

    my_params = lax.dynamic_slice_in_dim(params, slice_index * group, group, 0)
    spread_params = jnp.repeat(my_params, band_width, axis=1)
    fields = jnp.stack([diffusivity, velocity_x, velocity_y, source_shape])
    wide_fields = with_halo(fields, "space", depth)
    wide_coeffs = wide_fields[:3]
    global_rows = first_row - depth + jnp.arange(row_count + 2 * depth, dtype=jnp.int32)
    wide_inside = ((global_rows >= 0) & (global_rows < slabs)).astype(jnp.float32)[:, None]

    def step(values, low, step_size, forcing):
        n = values.shape[1]
        lo, hi = low + 1, low + n - 1
        q = None if forcing is None else forcing[:, lo:hi]
        return advance(values, wide_coeffs[:, lo:hi], wide_inside[lo:hi], step_size, q)

    by_group = state.reshape(slices, group, row_count, col_count)
    finished = []
    for member in range(group):
        mine = lax.all_to_all(by_group[:, member], "tm", 0, 0, tiled=True)
        wide_state = with_halo(mine, "space", depth)
        wide_forcing = wide_fields[3][None] * spread_params[member][None, None, :]
        current = wide_state
        coarse_part = step(wide_state, 0, coarse_dt, None)
        for section in range(FINE):
            current = step(current, section, FINE_DT, wide_forcing)
        coarse_part = coarse_part[:, FINE - 1 : FINE - 1 + current.shape[1]]
        running = current[0:1]
        results = [running[:, links : links + row_count]]
        for link in range(1, slices):
            correction = current[link : link + 1] - coarse_part[link : link + 1]
            stepped = step(running, FINE + link - 1, coarse_dt, None)
            running = correction[:, link : correction.shape[1] - link] + stepped
            results.append(running[:, links - link : links - link + row_count])
        done = jnp.concatenate(results)
        finished.append(lax.all_to_all(done, "tm", 0, 0, tiled=True))
    running = jnp.stack(finished, axis=1).reshape(members_here, row_count, col_count)
    new_states = running[None]

    local_cell = obs_cell[0] - first_row * col_count
    rows = local_cell // col_count
    cols = local_cell % col_count
    row_pick = (rows[:, None] == jnp.arange(row_count, dtype=jnp.int32)[None, :]).astype(jnp.float32)
    picked_rows = jnp.einsum("or,mrc->moc", row_pick, running, precision=lax.Precision.HIGHEST)
    at_col = lax.broadcasted_iota(jnp.int32, picked_rows.shape, 2) == cols[None, :, None]
    predicted = jnp.sum(jnp.where(at_col, picked_rows, 0.0), axis=2)
    every_pred = both_halves(predicted, "ens")
    every_param = both_halves(params, "ens")
    total = every_pred.shape[0]
    norm_factor = 1.0 / math.sqrt(total - 1)
    inv_spread = lax.rsqrt(obs_var[0])[None, :]
    pred_mean = jnp.mean(every_pred, axis=0, keepdims=True)
    anomaly = (every_pred - pred_mean) * (inv_spread * norm_factor)
    misfit = (obs_data[0][None, :] + obs_noise[0].T - every_pred) * inv_spread
    gram = jnp.dot(anomaly, anomaly.T, precision=lax.Precision.HIGHEST)
    cross = jnp.dot(anomaly, misfit.T, precision=lax.Precision.HIGHEST)
    sums = jnp.stack([gram, cross])
    sums = quad_sum(sums, "tm")
    sums = quad_sum(sums, "space")
    gram, cross = sums[0], sums[1]
    system = jnp.eye(total, dtype=jnp.float32) + gram
    factor = jnp.linalg.cholesky(system)
    weights = jax.scipy.linalg.cho_solve((factor, True), cross)
    param_anom = every_param - jnp.mean(every_param, axis=0)
    own_weights = lax.dynamic_slice_in_dim(
        weights, lax.axis_index("ens") * members_here, members_here, 1
    )
    new_params = (
        params + jnp.dot(own_weights.T, param_anom, precision=lax.Precision.HIGHEST) * norm_factor
    )
    return (new_states, new_params)


def solution(mesh):
    in_specs = (
        P("tm", "ens", "space", None),
        P("space", None),
        P("space", None),
        P("space", None),
        P("space", None),
        P("ens", None),
        P("tm", "space"),
        P("tm", "space"),
        P("tm", "space", None),
        P("tm", "space"),
    )
    out_specs = (P("tm", "ens", "space", None), P("ens", None))
    return jax.shard_map(
        per_device, mesh=mesh, in_specs=in_specs, out_specs=out_specs, check_vma=False
    )
```

```python
import math

import jax
import jax.numpy as jnp
from jax import lax
from jax.sharding import PartitionSpec as P

FINE = 4


FINE_DT = 0.25


def with_halo(cells, axis, width):
    count = lax.axis_size(axis)
    ends = count - 1
    head = cells[:, :width]
    tail = cells[:, cells.shape[1] - width :]
    return jnp.concatenate(
        [
            lax.ppermute(tail, axis, [(i, i + 1) for i in range(ends)]),
            cells,
            lax.ppermute(head, axis, [(i + 1, i) for i in range(ends)]),
        ],
        axis=1,
    )


def quad_sum(value, axis):
    count = lax.axis_size(axis)
    if count & (count - 1):
        return lax.psum(value, axis)
    bit = 1
    while bit < count:
        if bit * 4 <= count:
            near, far, both = (
                lax.ppermute(value, axis, [(i, i ^ (k * bit)) for i in range(count)])
                for k in (1, 2, 3)
            )
            value = (value + near) + (far + both)
            bit *= 4
        else:
            value = value + lax.ppermute(value, axis, [(i, i ^ bit) for i in range(count)])
            bit *= 2
    return value


def both_halves(value, axis):
    other = lax.ppermute(value, axis, [(0, 1), (1, 0)])
    first = lax.axis_index(axis) == 0
    return jnp.where(first, jnp.concatenate([value, other]), jnp.concatenate([other, value]))


def advance(values_in, coeffs, inside, step_size, forcing):
    middle = values_in[:, 1:-1, :]
    above_row = values_in[:, :-2, :]
    below_row = values_in[:, 2:, :]
    west_cell = jnp.pad(middle[:, :, :-1], ((0, 0), (0, 0), (1, 0)))
    east_cell = jnp.pad(middle[:, :, 1:], ((0, 0), (0, 0), (0, 1)))
    spread_term = coeffs[0] * (above_row + below_row + west_cell + east_cell - 4.0 * middle)
    tendency = (
        spread_term
        - coeffs[1] * (east_cell - west_cell) * 0.5
        - coeffs[2] * (below_row - above_row) * 0.5
    )
    if forcing is not None:
        tendency = tendency + forcing
    return (middle + step_size * tendency) * inside


def per_device(
    start_states,
    velocity_x,
    velocity_y,
    diffusivity,
    source_shape,
    params,
    obs_cell,
    obs_data,
    obs_noise,
    obs_var,
):
    coarse_dt = FINE_DT * FINE
    state = start_states[0]
    members_here, row_count, col_count = state.shape
    slabs = row_count * lax.axis_size("space")
    first_row = lax.axis_index("space") * row_count
    slice_index = lax.axis_index("tm")
    slices = lax.axis_size("tm")
    links = slices - 1
    depth = FINE + links
    group = members_here // slices
    band_width = col_count // params.shape[1]

    mine = lax.all_to_all(
        state.reshape(slices, group, row_count, col_count), "tm", 0, 0, tiled=True
    ).reshape(slices * group, row_count, col_count)
    my_params = lax.dynamic_slice_in_dim(params, slice_index * group, group, 0)
    spread_params = jnp.repeat(my_params, band_width, axis=1)

    fields = jnp.stack([diffusivity, velocity_x, velocity_y, source_shape])
    own = jnp.concatenate([mine, fields])
    wide = with_halo(own, "space", depth)
    count = slices * group
    global_rows = first_row - depth + jnp.arange(row_count + 2 * depth, dtype=jnp.int32)
    wide_inside = ((global_rows >= 0) & (global_rows < slabs)).astype(jnp.float32)[:, None]

    def block_steps(block, inside):
        states = block[:count]
        coeffs = block[count : count + 3]
        forcing = jnp.tile(block[count + 3][None] * spread_params[:, None, :], (slices, 1, 1))

        def step(values, off, step_size, q):
            lo, hi = off + 1, off + values.shape[1] - 1
            q = None if q is None else q[:, lo:hi]
            return advance(values, coeffs[:, lo:hi], inside[lo:hi], step_size, q)

        coarse = step(states, 0, coarse_dt, None)
        current = states
        for section in range(FINE):
            current = step(current, section, FINE_DT, forcing)
        return current, coarse[:, FINE - 1 : FINE - 1 + current.shape[1]]

    inner_fine, inner_coarse = block_steps(own, wide_inside[depth : depth + row_count])
    strip = depth + 2 * FINE
    strips = jnp.concatenate([wide[:, :strip], wide[:, -strip:]], axis=1)
    strips_inside = jnp.concatenate([wide_inside[:strip], wide_inside[-strip:]])
    edge_fine, edge_coarse = block_steps(strips, strips_inside)

    def stitch(edges, inner):
        return jnp.concatenate([edges[:, :depth], inner, edges[:, strip : strip + depth]], axis=1)

    current = stitch(edge_fine, inner_fine)
    coarse_part = stitch(edge_coarse, inner_coarse)
    wide_coeffs = wide[count : count + 3]

    def step(values, low, step_size, forcing):
        n = values.shape[1]
        lo, hi = low + 1, low + n - 1
        q = None if forcing is None else forcing[:, lo:hi]
        return advance(values, wide_coeffs[:, lo:hi], wide_inside[lo:hi], step_size, q)

    fine = current.reshape(slices, group, -1, col_count)
    coarse_part = coarse_part.reshape(slices, group, -1, col_count)
    running = fine[0]
    results = [running[:, links : links + row_count]]
    for link in range(1, slices):
        correction = fine[link] - coarse_part[link]
        stepped = step(running, FINE + link - 1, coarse_dt, None)
        running = correction[:, link : correction.shape[1] - link] + stepped
        results.append(running[:, links - link : links - link + row_count])
    done = jnp.stack(results)
    running = lax.all_to_all(done, "tm", 0, 0, tiled=True).reshape(
        members_here, row_count, col_count
    )
    new_states = running[None]

    local_cell = obs_cell[0] - first_row * col_count
    rows = local_cell // col_count
    cols = local_cell % col_count
    row_pick = (rows[:, None] == jnp.arange(row_count, dtype=jnp.int32)[None, :]).astype(jnp.float32)
    picked_rows = jnp.einsum("or,mrc->moc", row_pick, running, precision=lax.Precision.HIGHEST)
    at_col = lax.broadcasted_iota(jnp.int32, picked_rows.shape, 2) == cols[None, :, None]
    predicted = jnp.sum(jnp.where(at_col, picked_rows, 0.0), axis=2)
    every_pred = both_halves(predicted, "ens")
    every_param = both_halves(params, "ens")
    total = every_pred.shape[0]
    norm_factor = 1.0 / math.sqrt(total - 1)
    inv_spread = lax.rsqrt(obs_var[0])[None, :]
    pred_mean = jnp.mean(every_pred, axis=0, keepdims=True)
    anomaly = (every_pred - pred_mean) * (inv_spread * norm_factor)
    misfit = (obs_data[0][None, :] + obs_noise[0].T - every_pred) * inv_spread
    gram = jnp.dot(anomaly, anomaly.T, precision=lax.Precision.HIGHEST)
    cross = jnp.dot(anomaly, misfit.T, precision=lax.Precision.HIGHEST)
    sums = jnp.stack([gram, cross])
    sums = quad_sum(sums, "tm")
    sums = quad_sum(sums, "space")
    gram, cross = sums[0], sums[1]
    system = jnp.eye(total, dtype=jnp.float32) + gram
    factor = jnp.linalg.cholesky(system)
    weights = jax.scipy.linalg.cho_solve((factor, True), cross)
    param_anom = every_param - jnp.mean(every_param, axis=0)
    own_weights = lax.dynamic_slice_in_dim(
        weights, lax.axis_index("ens") * members_here, members_here, 1
    )
    new_params = (
        params + jnp.dot(own_weights.T, param_anom, precision=lax.Precision.HIGHEST) * norm_factor
    )
    return (new_states, new_params)


def solution(mesh):
    in_specs = (
        P("tm", "ens", "space", None),
        P("space", None),
        P("space", None),
        P("space", None),
        P("space", None),
        P("ens", None),
        P("tm", "space"),
        P("tm", "space"),
        P("tm", "space", None),
        P("tm", "space"),
    )
    out_specs = (P("tm", "ens", "space", None), P("ens", None))
    return jax.shard_map(
        per_device, mesh=mesh, in_specs=in_specs, out_specs=out_specs, check_vma=False
    )
```

```python
import math

import jax
import jax.numpy as jnp
from jax import lax
from jax.sharding import PartitionSpec as P

FINE = 4


FINE_DT = 0.25


def with_halo(cells, axis, width):
    count = lax.axis_size(axis)
    ends = count - 1
    head = cells[:, :width]
    tail = cells[:, cells.shape[1] - width :]
    return jnp.concatenate(
        [
            lax.ppermute(tail, axis, [(i, i + 1) for i in range(ends)]),
            cells,
            lax.ppermute(head, axis, [(i + 1, i) for i in range(ends)]),
        ],
        axis=1,
    )


def quad_sum(value, axis):
    count = lax.axis_size(axis)
    if count & (count - 1):
        return lax.psum(value, axis)
    bit = 1
    while bit < count:
        if bit * 4 <= count:
            near, far, both = (
                lax.ppermute(value, axis, [(i, i ^ (k * bit)) for i in range(count)])
                for k in (1, 2, 3)
            )
            value = (value + near) + (far + both)
            bit *= 4
        else:
            value = value + lax.ppermute(value, axis, [(i, i ^ bit) for i in range(count)])
            bit *= 2
    return value


def both_halves(value, axis):
    other = lax.ppermute(value, axis, [(0, 1), (1, 0)])
    first = lax.axis_index(axis) == 0
    return jnp.where(first, jnp.concatenate([value, other]), jnp.concatenate([other, value]))


def advance(values_in, coeffs, inside, step_size, forcing):
    middle = values_in[:, 1:-1, :]
    above_row = values_in[:, :-2, :]
    below_row = values_in[:, 2:, :]
    west_cell = jnp.pad(middle[:, :, :-1], ((0, 0), (0, 0), (1, 0)))
    east_cell = jnp.pad(middle[:, :, 1:], ((0, 0), (0, 0), (0, 1)))
    spread_term = coeffs[0] * (above_row + below_row + west_cell + east_cell - 4.0 * middle)
    tendency = (
        spread_term
        - coeffs[1] * (east_cell - west_cell) * 0.5
        - coeffs[2] * (below_row - above_row) * 0.5
    )
    if forcing is not None:
        tendency = tendency + forcing
    return (middle + step_size * tendency) * inside


def per_device(
    start_states,
    velocity_x,
    velocity_y,
    diffusivity,
    source_shape,
    params,
    obs_cell,
    obs_data,
    obs_noise,
    obs_var,
):
    coarse_dt = FINE_DT * FINE
    state = start_states[0]
    members_here, row_count, col_count = state.shape
    slabs = row_count * lax.axis_size("space")
    first_row = lax.axis_index("space") * row_count
    slice_index = lax.axis_index("tm")
    slices = lax.axis_size("tm")
    links = slices - 1
    depth = FINE + links
    group = members_here // slices
    band_width = col_count // params.shape[1]

    mine = lax.all_to_all(
        state.reshape(slices, group, row_count, col_count), "tm", 0, 0, tiled=True
    ).reshape(slices * group, row_count, col_count)
    my_params = lax.dynamic_slice_in_dim(params, slice_index * group, group, 0)
    spread_params = jnp.repeat(my_params, band_width, axis=1)

    fields = jnp.stack([diffusivity, velocity_x, velocity_y, source_shape])
    count = slices * group
    both = jnp.concatenate([state, fields])
    spaces = lax.axis_size("space")
    from_above = lax.ppermute(
        both[:, row_count - depth :], "space", [(i, i + 1) for i in range(spaces - 1)]
    )
    from_below = lax.ppermute(both[:, :depth], "space", [(i + 1, i) for i in range(spaces - 1)])
    edge_states = jnp.concatenate([from_above[:members_here], from_below[:members_here]], axis=1)
    edge_states = lax.all_to_all(
        edge_states.reshape(slices, group, 2 * depth, col_count), "tm", 0, 0, tiled=True
    ).reshape(count, 2 * depth, col_count)
    above = jnp.concatenate([edge_states[:, :depth], from_above[members_here:]])
    below = jnp.concatenate([edge_states[:, depth:], from_below[members_here:]])
    own = jnp.concatenate([mine, fields])
    wide_fields = jnp.concatenate([from_above[members_here:], fields, from_below[members_here:]], axis=1)
    global_rows = first_row - depth + jnp.arange(row_count + 2 * depth, dtype=jnp.int32)
    wide_inside = ((global_rows >= 0) & (global_rows < slabs)).astype(jnp.float32)[:, None]

    def block_steps(block, inside):
        states = block[:count]
        coeffs = block[count : count + 3]
        forcing = jnp.tile(block[count + 3][None] * spread_params[:, None, :], (slices, 1, 1))

        def step(values, off, step_size, q):
            lo, hi = off + 1, off + values.shape[1] - 1
            q = None if q is None else q[:, lo:hi]
            return advance(values, coeffs[:, lo:hi], inside[lo:hi], step_size, q)

        coarse = step(states, 0, coarse_dt, None)
        current = states
        for section in range(FINE):
            current = step(current, section, FINE_DT, forcing)
        return current, coarse[:, FINE - 1 : FINE - 1 + current.shape[1]]

    inner_fine, inner_coarse = block_steps(own, wide_inside[depth : depth + row_count])
    strip = depth + 2 * FINE
    strips = jnp.concatenate(
        [above, own[:, : strip - depth], own[:, row_count - (strip - depth) :], below], axis=1
    )
    strips_inside = jnp.concatenate([wide_inside[:strip], wide_inside[-strip:]])
    edge_fine, edge_coarse = block_steps(strips, strips_inside)

    def stitch(edges, inner):
        return jnp.concatenate([edges[:, :depth], inner, edges[:, strip : strip + depth]], axis=1)

    current = stitch(edge_fine, inner_fine)
    coarse_part = stitch(edge_coarse, inner_coarse)
    wide_coeffs = wide_fields[:3]

    def step(values, low, step_size, forcing):
        n = values.shape[1]
        lo, hi = low + 1, low + n - 1
        q = None if forcing is None else forcing[:, lo:hi]
        return advance(values, wide_coeffs[:, lo:hi], wide_inside[lo:hi], step_size, q)

    fine = current.reshape(slices, group, -1, col_count)
    coarse_part = coarse_part.reshape(slices, group, -1, col_count)
    running = fine[0]
    results = [running[:, links : links + row_count]]
    for link in range(1, slices):
        correction = fine[link] - coarse_part[link]
        stepped = step(running, FINE + link - 1, coarse_dt, None)
        running = correction[:, link : correction.shape[1] - link] + stepped
        results.append(running[:, links - link : links - link + row_count])
    done = jnp.stack(results)
    running = lax.all_to_all(done, "tm", 0, 0, tiled=True).reshape(
        members_here, row_count, col_count
    )
    new_states = running[None]

    local_cell = obs_cell[0] - first_row * col_count
    rows = local_cell // col_count
    cols = local_cell % col_count
    row_pick = (rows[:, None] == jnp.arange(row_count, dtype=jnp.int32)[None, :]).astype(jnp.float32)
    picked_rows = jnp.einsum("or,mrc->moc", row_pick, running, precision=lax.Precision.HIGHEST)
    at_col = lax.broadcasted_iota(jnp.int32, picked_rows.shape, 2) == cols[None, :, None]
    predicted = jnp.sum(jnp.where(at_col, picked_rows, 0.0), axis=2)
    every_pred = both_halves(predicted, "ens")
    every_param = both_halves(params, "ens")
    total = every_pred.shape[0]
    norm_factor = 1.0 / math.sqrt(total - 1)
    inv_spread = lax.rsqrt(obs_var[0])[None, :]
    pred_mean = jnp.mean(every_pred, axis=0, keepdims=True)
    anomaly = (every_pred - pred_mean) * (inv_spread * norm_factor)
    misfit = (obs_data[0][None, :] + obs_noise[0].T - every_pred) * inv_spread
    gram = jnp.dot(anomaly, anomaly.T, precision=lax.Precision.HIGHEST)
    cross = jnp.dot(anomaly, misfit.T, precision=lax.Precision.HIGHEST)
    sums = jnp.stack([gram, cross])
    sums = quad_sum(sums, "tm")
    sums = quad_sum(sums, "space")
    gram, cross = sums[0], sums[1]
    system = jnp.eye(total, dtype=jnp.float32) + gram
    factor = jnp.linalg.cholesky(system)
    weights = jax.scipy.linalg.cho_solve((factor, True), cross)
    param_anom = every_param - jnp.mean(every_param, axis=0)
    own_weights = lax.dynamic_slice_in_dim(
        weights, lax.axis_index("ens") * members_here, members_here, 1
    )
    new_params = (
        params + jnp.dot(own_weights.T, param_anom, precision=lax.Precision.HIGHEST) * norm_factor
    )
    return (new_states, new_params)


def solution(mesh):
    in_specs = (
        P("tm", "ens", "space", None),
        P("space", None),
        P("space", None),
        P("space", None),
        P("space", None),
        P("ens", None),
        P("tm", "space"),
        P("tm", "space"),
        P("tm", "space", None),
        P("tm", "space"),
    )
    out_specs = (P("tm", "ens", "space", None), P("ens", None))
    return jax.shard_map(
        per_device, mesh=mesh, in_specs=in_specs, out_specs=out_specs, check_vma=False
    )
```

```python
import math

import jax
import jax.numpy as jnp
from jax import lax
from jax.sharding import PartitionSpec as P

FINE = 4


FINE_DT = 0.25


def with_halo(cells, axis, width):
    count = lax.axis_size(axis)
    ends = count - 1
    head = cells[:, :width]
    tail = cells[:, cells.shape[1] - width :]
    return jnp.concatenate(
        [
            lax.ppermute(tail, axis, [(i, i + 1) for i in range(ends)]),
            cells,
            lax.ppermute(head, axis, [(i + 1, i) for i in range(ends)]),
        ],
        axis=1,
    )


def quad_sum(value, axis):
    count = lax.axis_size(axis)
    if count & (count - 1):
        return lax.psum(value, axis)
    bit = 1
    while bit < count:
        if bit * 4 <= count:
            near, far, both = (
                lax.ppermute(value, axis, [(i, i ^ (k * bit)) for i in range(count)])
                for k in (1, 2, 3)
            )
            value = (value + near) + (far + both)
            bit *= 4
        else:
            value = value + lax.ppermute(value, axis, [(i, i ^ bit) for i in range(count)])
            bit *= 2
    return value


def both_halves(value, axis):
    other = lax.ppermute(value, axis, [(0, 1), (1, 0)])
    first = lax.axis_index(axis) == 0
    return jnp.where(first, jnp.concatenate([value, other]), jnp.concatenate([other, value]))


def advance(values_in, coeffs, inside, step_size, forcing):
    middle = values_in[:, 1:-1, :]
    above_row = values_in[:, :-2, :]
    below_row = values_in[:, 2:, :]
    west_cell = jnp.pad(middle[:, :, :-1], ((0, 0), (0, 0), (1, 0)))
    east_cell = jnp.pad(middle[:, :, 1:], ((0, 0), (0, 0), (0, 1)))
    spread_term = coeffs[0] * (above_row + below_row + west_cell + east_cell - 4.0 * middle)
    tendency = (
        spread_term
        - coeffs[1] * (east_cell - west_cell) * 0.5
        - coeffs[2] * (below_row - above_row) * 0.5
    )
    if forcing is not None:
        tendency = tendency + forcing
    return (middle + step_size * tendency) * inside


def per_device(
    start_states,
    velocity_x,
    velocity_y,
    diffusivity,
    source_shape,
    params,
    obs_cell,
    obs_data,
    obs_noise,
    obs_var,
):
    coarse_dt = FINE_DT * FINE
    state = start_states[0]
    members_here, row_count, col_count = state.shape
    slabs = row_count * lax.axis_size("space")
    first_row = lax.axis_index("space") * row_count
    slice_index = lax.axis_index("tm")
    slices = lax.axis_size("tm")
    links = slices - 1
    depth = FINE + links
    group = members_here // slices
    band_width = col_count // params.shape[1]

    mine = lax.all_to_all(
        state.reshape(slices, group, row_count, col_count), "tm", 0, 0, tiled=True
    ).reshape(slices * group, row_count, col_count)
    my_params = lax.dynamic_slice_in_dim(params, slice_index * group, group, 0)
    spread_params = jnp.repeat(my_params, band_width, axis=1)

    fields = jnp.stack([diffusivity, velocity_x, velocity_y, source_shape])
    own = jnp.concatenate([mine, fields])
    wide_fields = with_halo(fields, "space", depth)
    wide = jnp.concatenate([with_halo(mine, "space", depth), wide_fields])
    count = slices * group
    global_rows = first_row - depth + jnp.arange(row_count + 2 * depth, dtype=jnp.int32)
    wide_inside = ((global_rows >= 0) & (global_rows < slabs)).astype(jnp.float32)[:, None]

    def block_steps(block, inside):
        states = block[:count]
        coeffs = block[count : count + 3]
        forcing = jnp.tile(block[count + 3][None] * spread_params[:, None, :], (slices, 1, 1))

        def step(values, off, step_size, q):
            lo, hi = off + 1, off + values.shape[1] - 1
            q = None if q is None else q[:, lo:hi]
            return advance(values, coeffs[:, lo:hi], inside[lo:hi], step_size, q)

        coarse = step(states, 0, coarse_dt, None)
        current = states
        for section in range(FINE):
            current = step(current, section, FINE_DT, forcing)
        return current, coarse[:, FINE - 1 : FINE - 1 + current.shape[1]]

    inner_fine, inner_coarse = block_steps(own, wide_inside[depth : depth + row_count])
    strip = depth + 2 * FINE
    strips = jnp.concatenate([wide[:, :strip], wide[:, -strip:]], axis=1)
    strips_inside = jnp.concatenate([wide_inside[:strip], wide_inside[-strip:]])
    edge_fine, edge_coarse = block_steps(strips, strips_inside)

    def stitch(edges, inner):
        return jnp.concatenate([edges[:, :depth], inner, edges[:, strip : strip + depth]], axis=1)

    current = stitch(edge_fine, inner_fine)
    coarse_part = stitch(edge_coarse, inner_coarse)
    wide_coeffs = wide[count : count + 3]

    def step(values, low, step_size, forcing):
        n = values.shape[1]
        lo, hi = low + 1, low + n - 1
        q = None if forcing is None else forcing[:, lo:hi]
        return advance(values, wide_coeffs[:, lo:hi], wide_inside[lo:hi], step_size, q)

    fine = current.reshape(slices, group, -1, col_count)
    coarse_part = coarse_part.reshape(slices, group, -1, col_count)
    running = fine[0]
    results = [running[:, links : links + row_count]]
    for link in range(1, slices):
        correction = fine[link] - coarse_part[link]
        stepped = step(running, FINE + link - 1, coarse_dt, None)
        running = correction[:, link : correction.shape[1] - link] + stepped
        results.append(running[:, links - link : links - link + row_count])
    done = jnp.stack(results)
    running = lax.all_to_all(done, "tm", 0, 0, tiled=True).reshape(
        members_here, row_count, col_count
    )
    new_states = running[None]

    local_cell = obs_cell[0] - first_row * col_count
    rows = local_cell // col_count
    cols = local_cell % col_count
    row_pick = (rows[:, None] == jnp.arange(row_count, dtype=jnp.int32)[None, :]).astype(jnp.float32)
    picked_rows = jnp.einsum("or,mrc->moc", row_pick, running, precision=lax.Precision.HIGHEST)
    at_col = lax.broadcasted_iota(jnp.int32, picked_rows.shape, 2) == cols[None, :, None]
    predicted = jnp.sum(jnp.where(at_col, picked_rows, 0.0), axis=2)
    every_pred = both_halves(predicted, "ens")
    every_param = both_halves(params, "ens")
    total = every_pred.shape[0]
    norm_factor = 1.0 / math.sqrt(total - 1)
    inv_spread = lax.rsqrt(obs_var[0])[None, :]
    pred_mean = jnp.mean(every_pred, axis=0, keepdims=True)
    anomaly = (every_pred - pred_mean) * (inv_spread * norm_factor)
    misfit = (obs_data[0][None, :] + obs_noise[0].T - every_pred) * inv_spread
    gram = jnp.dot(anomaly, anomaly.T, precision=lax.Precision.HIGHEST)
    cross = jnp.dot(anomaly, misfit.T, precision=lax.Precision.HIGHEST)
    sums = jnp.stack([gram, cross])
    sums = quad_sum(sums, "tm")
    sums = quad_sum(sums, "space")
    gram, cross = sums[0], sums[1]
    system = jnp.eye(total, dtype=jnp.float32) + gram
    factor = jnp.linalg.cholesky(system)
    weights = jax.scipy.linalg.cho_solve((factor, True), cross)
    param_anom = every_param - jnp.mean(every_param, axis=0)
    own_weights = lax.dynamic_slice_in_dim(
        weights, lax.axis_index("ens") * members_here, members_here, 1
    )
    new_params = (
        params + jnp.dot(own_weights.T, param_anom, precision=lax.Precision.HIGHEST) * norm_factor
    )
    return (new_states, new_params)


def solution(mesh):
    in_specs = (
        P("tm", "ens", "space", None),
        P("space", None),
        P("space", None),
        P("space", None),
        P("space", None),
        P("ens", None),
        P("tm", "space"),
        P("tm", "space"),
        P("tm", "space", None),
        P("tm", "space"),
    )
    out_specs = (P("tm", "ens", "space", None), P("ens", None))
    return jax.shard_map(
        per_device, mesh=mesh, in_specs=in_specs, out_specs=out_specs, check_vma=False
    )
```

```python
import math

import jax
import jax.numpy as jnp
from jax import lax
from jax.sharding import PartitionSpec as P

FINE = 4


FINE_DT = 0.25


def with_halo(cells, axis, width):
    count = lax.axis_size(axis)
    ends = count - 1
    head = cells[:, :width]
    tail = cells[:, cells.shape[1] - width :]
    return jnp.concatenate(
        [
            lax.ppermute(tail, axis, [(i, i + 1) for i in range(ends)]),
            cells,
            lax.ppermute(head, axis, [(i + 1, i) for i in range(ends)]),
        ],
        axis=1,
    )


def quad_sum(value, axis):
    count = lax.axis_size(axis)
    if count & (count - 1):
        return lax.psum(value, axis)
    bit = 1
    while bit < count:
        if bit * 4 <= count:
            near, far, both = (
                lax.ppermute(value, axis, [(i, i ^ (k * bit)) for i in range(count)])
                for k in (1, 2, 3)
            )
            value = (value + near) + (far + both)
            bit *= 4
        else:
            value = value + lax.ppermute(value, axis, [(i, i ^ bit) for i in range(count)])
            bit *= 2
    return value


def both_halves(value, axis):
    other = lax.ppermute(value, axis, [(0, 1), (1, 0)])
    first = lax.axis_index(axis) == 0
    return jnp.where(first, jnp.concatenate([value, other]), jnp.concatenate([other, value]))


def advance(values_in, coeffs, inside, step_size, forcing):
    middle = values_in[:, 1:-1, :]
    above_row = values_in[:, :-2, :]
    below_row = values_in[:, 2:, :]
    west_cell = jnp.pad(middle[:, :, :-1], ((0, 0), (0, 0), (1, 0)))
    east_cell = jnp.pad(middle[:, :, 1:], ((0, 0), (0, 0), (0, 1)))
    spread_term = coeffs[0] * (above_row + below_row + west_cell + east_cell - 4.0 * middle)
    tendency = (
        spread_term
        - coeffs[1] * (east_cell - west_cell) * 0.5
        - coeffs[2] * (below_row - above_row) * 0.5
    )
    if forcing is not None:
        tendency = tendency + forcing
    return (middle + step_size * tendency) * inside


def per_device(
    start_states,
    velocity_x,
    velocity_y,
    diffusivity,
    source_shape,
    params,
    obs_cell,
    obs_data,
    obs_noise,
    obs_var,
):
    coarse_dt = FINE_DT * FINE
    state = start_states[0]
    members_here, row_count, col_count = state.shape
    slabs = row_count * lax.axis_size("space")
    first_row = lax.axis_index("space") * row_count
    slice_index = lax.axis_index("tm")
    slices = lax.axis_size("tm")
    links = slices - 1
    depth = FINE + links
    group = members_here // slices
    band_width = col_count // params.shape[1]

    mine = lax.all_to_all(
        state.reshape(slices, group, row_count, col_count), "tm", 0, 0, tiled=True
    ).reshape(slices * group, row_count, col_count)
    my_params = lax.dynamic_slice_in_dim(params, slice_index * group, group, 0)
    spread_params = jnp.repeat(my_params, band_width, axis=1)

    fields = jnp.stack([diffusivity, velocity_x, velocity_y, source_shape])
    own = jnp.concatenate([mine, fields])
    wide_fields = with_halo(fields, "space", depth)
    wide = jnp.concatenate([with_halo(mine, "space", depth), wide_fields])
    count = slices * group
    global_rows = first_row - depth + jnp.arange(row_count + 2 * depth, dtype=jnp.int32)
    wide_inside = ((global_rows >= 0) & (global_rows < slabs)).astype(jnp.float32)[:, None]

    def block_steps(block, inside):
        states = block[:count]
        coeffs = block[count : count + 3]
        forcing = jnp.tile(block[count + 3][None] * spread_params[:, None, :], (slices, 1, 1))

        def step(values, off, step_size, q):
            lo, hi = off + 1, off + values.shape[1] - 1
            q = None if q is None else q[:, lo:hi]
            return advance(values, coeffs[:, lo:hi], inside[lo:hi], step_size, q)

        coarse = step(states, 0, coarse_dt, None)
        current = states
        for section in range(FINE):
            current = step(current, section, FINE_DT, forcing)
        return current, coarse[:, FINE - 1 : FINE - 1 + current.shape[1]]

    inner_fine, inner_coarse = block_steps(own, wide_inside[depth : depth + row_count])
    strip = depth + 2 * FINE
    strips = jnp.concatenate([wide[:, :strip], wide[:, -strip:]], axis=1)
    strips_inside = jnp.concatenate([wide_inside[:strip], wide_inside[-strip:]])
    edge_fine, edge_coarse = block_steps(strips, strips_inside)

    def stitch(edges, inner):
        return jnp.concatenate([edges[:, :depth], inner, edges[:, strip : strip + depth]], axis=1)

    current = stitch(edge_fine, inner_fine)
    coarse_part = stitch(edge_coarse, inner_coarse)
    wide_coeffs = wide[count : count + 3]

    def step(values, low, step_size, forcing):
        n = values.shape[1]
        lo, hi = low + 1, low + n - 1
        q = None if forcing is None else forcing[:, lo:hi]
        return advance(values, wide_coeffs[:, lo:hi], wide_inside[lo:hi], step_size, q)

    fine = current.reshape(slices, group, -1, col_count)
    coarse_part = coarse_part.reshape(slices, group, -1, col_count)
    running = fine[0]
    done = jnp.zeros((slices, group, row_count, col_count), jnp.float32)
    done = done.at[0].set(running[:, links : links + row_count])
    for link in range(1, slices):
        correction = fine[link] - coarse_part[link]
        stepped = step(running, FINE + link - 1, coarse_dt, None)
        running = correction[:, link : correction.shape[1] - link] + stepped
        done = done.at[link].set(running[:, links - link : links - link + row_count])
    running = lax.all_to_all(done, "tm", 0, 0, tiled=True).reshape(
        members_here, row_count, col_count
    )
    new_states = running[None]

    local_cell = obs_cell[0] - first_row * col_count
    rows = local_cell // col_count
    cols = local_cell % col_count
    row_pick = (rows[:, None] == jnp.arange(row_count, dtype=jnp.int32)[None, :]).astype(jnp.float32)
    picked_rows = jnp.einsum("or,mrc->moc", row_pick, running, precision=lax.Precision.HIGHEST)
    at_col = lax.broadcasted_iota(jnp.int32, picked_rows.shape, 2) == cols[None, :, None]
    predicted = jnp.sum(jnp.where(at_col, picked_rows, 0.0), axis=2)
    every_pred = both_halves(predicted, "ens")
    every_param = both_halves(params, "ens")
    total = every_pred.shape[0]
    norm_factor = 1.0 / math.sqrt(total - 1)
    inv_spread = lax.rsqrt(obs_var[0])[None, :]
    pred_mean = jnp.mean(every_pred, axis=0, keepdims=True)
    anomaly = (every_pred - pred_mean) * (inv_spread * norm_factor)
    misfit = (obs_data[0][None, :] + obs_noise[0].T - every_pred) * inv_spread
    gram = jnp.dot(anomaly, anomaly.T, precision=lax.Precision.HIGHEST)
    cross = jnp.dot(anomaly, misfit.T, precision=lax.Precision.HIGHEST)
    sums = jnp.stack([gram, cross])
    sums = quad_sum(sums, "tm")
    sums = quad_sum(sums, "space")
    gram, cross = sums[0], sums[1]
    system = jnp.eye(total, dtype=jnp.float32) + gram
    factor = jnp.linalg.cholesky(system)
    weights = jax.scipy.linalg.cho_solve((factor, True), cross)
    param_anom = every_param - jnp.mean(every_param, axis=0)
    own_weights = lax.dynamic_slice_in_dim(
        weights, lax.axis_index("ens") * members_here, members_here, 1
    )
    new_params = (
        params + jnp.dot(own_weights.T, param_anom, precision=lax.Precision.HIGHEST) * norm_factor
    )
    return (new_states, new_params)


def solution(mesh):
    in_specs = (
        P("tm", "ens", "space", None),
        P("space", None),
        P("space", None),
        P("space", None),
        P("space", None),
        P("ens", None),
        P("tm", "space"),
        P("tm", "space"),
        P("tm", "space", None),
        P("tm", "space"),
    )
    out_specs = (P("tm", "ens", "space", None), P("ens", None))
    return jax.shard_map(
        per_device, mesh=mesh, in_specs=in_specs, out_specs=out_specs, check_vma=False
    )
```

```python
import math

import jax
import jax.numpy as jnp
from jax import lax
from jax.sharding import PartitionSpec as P

FINE = 4


FINE_DT = 0.25


def with_halo(cells, axis, width):
    count = lax.axis_size(axis)
    ends = count - 1
    head = cells[:, :width]
    tail = cells[:, cells.shape[1] - width :]
    return jnp.concatenate(
        [
            lax.ppermute(tail, axis, [(i, i + 1) for i in range(ends)]),
            cells,
            lax.ppermute(head, axis, [(i + 1, i) for i in range(ends)]),
        ],
        axis=1,
    )


def quad_sum(value, axis):
    count = lax.axis_size(axis)
    if count & (count - 1):
        return lax.psum(value, axis)
    bit = 1
    while bit < count:
        if bit * 4 <= count:
            near, far, both = (
                lax.ppermute(value, axis, [(i, i ^ (k * bit)) for i in range(count)])
                for k in (1, 2, 3)
            )
            value = (value + near) + (far + both)
            bit *= 4
        else:
            value = value + lax.ppermute(value, axis, [(i, i ^ bit) for i in range(count)])
            bit *= 2
    return value


def both_halves(value, axis):
    other = lax.ppermute(value, axis, [(0, 1), (1, 0)])
    first = lax.axis_index(axis) == 0
    return jnp.where(first, jnp.concatenate([value, other]), jnp.concatenate([other, value]))


def advance(values_in, coeffs, inside, step_size, forcing):
    middle = values_in[:, 1:-1, :]
    above_row = values_in[:, :-2, :]
    below_row = values_in[:, 2:, :]
    west_cell = jnp.pad(middle[:, :, :-1], ((0, 0), (0, 0), (1, 0)))
    east_cell = jnp.pad(middle[:, :, 1:], ((0, 0), (0, 0), (0, 1)))
    spread_term = coeffs[0] * (above_row + below_row + west_cell + east_cell - 4.0 * middle)
    tendency = (
        spread_term
        - coeffs[1] * (east_cell - west_cell) * 0.5
        - coeffs[2] * (below_row - above_row) * 0.5
    )
    if forcing is not None:
        tendency = tendency + forcing
    return (middle + step_size * tendency) * inside


def per_device(
    start_states,
    velocity_x,
    velocity_y,
    diffusivity,
    source_shape,
    params,
    obs_cell,
    obs_data,
    obs_noise,
    obs_var,
):
    coarse_dt = FINE_DT * FINE
    state = start_states[0]
    members_here, row_count, col_count = state.shape
    slabs = row_count * lax.axis_size("space")
    first_row = lax.axis_index("space") * row_count
    slice_index = lax.axis_index("tm")
    slices = lax.axis_size("tm")
    links = slices - 1
    depth = FINE + links
    group = members_here // slices
    band_width = col_count // params.shape[1]

    mine = lax.all_to_all(
        state.reshape(slices, group, row_count, col_count), "tm", 0, 0, tiled=True
    ).reshape(slices * group, row_count, col_count)
    my_params = lax.dynamic_slice_in_dim(params, slice_index * group, group, 0)
    spread_params = jnp.repeat(my_params, band_width, axis=1)

    fields = jnp.stack([diffusivity, velocity_x, velocity_y, source_shape])
    own = jnp.concatenate([mine, fields])
    wide_fields = with_halo(fields, "space", depth)
    wide = jnp.concatenate([with_halo(mine, "space", depth), wide_fields])
    count = slices * group
    global_rows = first_row - depth + jnp.arange(row_count + 2 * depth, dtype=jnp.int32)
    wide_inside = ((global_rows >= 0) & (global_rows < slabs)).astype(jnp.float32)[:, None]

    def block_steps(block, inside):
        states = block[:count]
        coeffs = block[count : count + 3]
        forcing = jnp.tile(block[count + 3][None] * spread_params[:, None, :], (slices, 1, 1))

        def step(values, off, step_size, q):
            lo, hi = off + 1, off + values.shape[1] - 1
            q = None if q is None else q[:, lo:hi]
            return advance(values, coeffs[:, lo:hi], inside[lo:hi], step_size, q)

        coarse = step(states, 0, coarse_dt, None)
        current = states
        for section in range(FINE):
            current = step(current, section, FINE_DT, forcing)
        return current, coarse[:, FINE - 1 : FINE - 1 + current.shape[1]]

    inner_fine, inner_coarse = block_steps(own, wide_inside[depth : depth + row_count])
    strip = depth + 2 * FINE
    strips = jnp.concatenate([wide[:, :strip], wide[:, -strip:]], axis=1)
    strips_inside = jnp.concatenate([wide_inside[:strip], wide_inside[-strip:]])
    edge_fine, edge_coarse = block_steps(strips, strips_inside)

    def stitch(edges, inner):
        return jnp.concatenate([edges[:, :depth], inner, edges[:, strip : strip + depth]], axis=1)

    current = stitch(edge_fine, inner_fine)
    coarse_part = stitch(edge_coarse, inner_coarse)
    wide_coeffs = wide[count : count + 3]

    def step(values, low, step_size, forcing):
        n = values.shape[1]
        lo, hi = low + 1, low + n - 1
        q = None if forcing is None else forcing[:, lo:hi]
        return advance(values, wide_coeffs[:, lo:hi], wide_inside[lo:hi], step_size, q)

    fine = current.reshape(slices, group, -1, col_count)
    coarse_part = coarse_part.reshape(slices, group, -1, col_count)
    running = fine[0]
    results = [running[:, links : links + row_count]]
    for link in range(1, slices):
        correction = fine[link] - coarse_part[link]
        stepped = step(running, FINE + link - 1, coarse_dt, None)
        running = correction[:, link : correction.shape[1] - link] + stepped
        results.append(running[:, links - link : links - link + row_count])
    done = jnp.stack(results)
    running = lax.all_to_all(done, "tm", 0, 0, tiled=True).reshape(
        members_here, row_count, col_count
    )
    new_states = running[None]

    local_cell = obs_cell[0] - first_row * col_count
    rows = local_cell // col_count
    cols = local_cell % col_count
    row_pick = (rows[:, None] == jnp.arange(row_count, dtype=jnp.int32)[None, :]).astype(jnp.float32)
    picked_rows = jnp.einsum("or,mrc->moc", row_pick, running, precision=lax.Precision.HIGHEST)
    at_col = lax.broadcasted_iota(jnp.int32, picked_rows.shape, 2) == cols[None, :, None]
    predicted = jnp.sum(jnp.where(at_col, picked_rows, 0.0), axis=2)
    every_pred = both_halves(predicted, "ens")
    every_param = both_halves(params, "ens")
    total = every_pred.shape[0]
    norm_factor = 1.0 / math.sqrt(total - 1)
    inv_spread = lax.rsqrt(obs_var[0])[None, :]
    pred_mean = jnp.mean(every_pred, axis=0, keepdims=True)
    anomaly = (every_pred - pred_mean) * (inv_spread * norm_factor)
    misfit = (obs_data[0][None, :] + obs_noise[0].T - every_pred) * inv_spread
    gram = jnp.dot(anomaly, anomaly.T, precision=lax.Precision.HIGHEST)
    cross = jnp.dot(anomaly, misfit.T, precision=lax.Precision.HIGHEST)
    sums = jnp.stack([gram, cross])
    sums = quad_sum(sums, "space")
    sums = quad_sum(sums, "tm")
    gram, cross = sums[0], sums[1]
    system = jnp.eye(total, dtype=jnp.float32) + gram
    factor = jnp.linalg.cholesky(system)
    weights = jax.scipy.linalg.cho_solve((factor, True), cross)
    param_anom = every_param - jnp.mean(every_param, axis=0)
    own_weights = lax.dynamic_slice_in_dim(
        weights, lax.axis_index("ens") * members_here, members_here, 1
    )
    new_params = (
        params + jnp.dot(own_weights.T, param_anom, precision=lax.Precision.HIGHEST) * norm_factor
    )
    return (new_states, new_params)


def solution(mesh):
    in_specs = (
        P("tm", "ens", "space", None),
        P("space", None),
        P("space", None),
        P("space", None),
        P("space", None),
        P("ens", None),
        P("tm", "space"),
        P("tm", "space"),
        P("tm", "space", None),
        P("tm", "space"),
    )
    out_specs = (P("tm", "ens", "space", None), P("ens", None))
    return jax.shard_map(
        per_device, mesh=mesh, in_specs=in_specs, out_specs=out_specs, check_vma=False
    )
```

```python
import math

import jax
import jax.numpy as jnp
from jax import lax
from jax.sharding import PartitionSpec as P

FINE = 4


FINE_DT = 0.25


def with_halo(cells, axis, width):
    count = lax.axis_size(axis)
    ends = count - 1
    head = cells[:, :width]
    tail = cells[:, cells.shape[1] - width :]
    return jnp.concatenate(
        [
            lax.ppermute(tail, axis, [(i, i + 1) for i in range(ends)]),
            cells,
            lax.ppermute(head, axis, [(i + 1, i) for i in range(ends)]),
        ],
        axis=1,
    )


def quad_sum(value, axis):
    count = lax.axis_size(axis)
    if count & (count - 1):
        return lax.psum(value, axis)
    bit = 1
    while bit < count:
        if bit * 4 <= count:
            near, far, both = (
                lax.ppermute(value, axis, [(i, i ^ (k * bit)) for i in range(count)])
                for k in (1, 2, 3)
            )
            value = (value + near) + (far + both)
            bit *= 4
        else:
            value = value + lax.ppermute(value, axis, [(i, i ^ bit) for i in range(count)])
            bit *= 2
    return value


def both_halves(value, axis):
    other = lax.ppermute(value, axis, [(0, 1), (1, 0)])
    first = lax.axis_index(axis) == 0
    return jnp.where(first, jnp.concatenate([value, other]), jnp.concatenate([other, value]))


def advance(values_in, coeffs, inside, step_size, forcing):
    middle = values_in[:, 1:-1, :]
    above_row = values_in[:, :-2, :]
    below_row = values_in[:, 2:, :]
    west_cell = jnp.pad(middle[:, :, :-1], ((0, 0), (0, 0), (1, 0)))
    east_cell = jnp.pad(middle[:, :, 1:], ((0, 0), (0, 0), (0, 1)))
    spread_term = coeffs[0] * (above_row + below_row + west_cell + east_cell - 4.0 * middle)
    tendency = (
        spread_term
        - coeffs[1] * (east_cell - west_cell) * 0.5
        - coeffs[2] * (below_row - above_row) * 0.5
    )
    if forcing is not None:
        tendency = tendency + forcing
    return (middle + step_size * tendency) * inside


def per_device(
    start_states,
    velocity_x,
    velocity_y,
    diffusivity,
    source_shape,
    params,
    obs_cell,
    obs_data,
    obs_noise,
    obs_var,
):
    coarse_dt = FINE_DT * FINE
    state = start_states[0]
    members_here, row_count, col_count = state.shape
    slabs = row_count * lax.axis_size("space")
    first_row = lax.axis_index("space") * row_count
    slice_index = lax.axis_index("tm")
    slices = lax.axis_size("tm")
    links = slices - 1
    depth = FINE + links
    group = members_here // slices
    band_width = col_count // params.shape[1]

    mine = lax.all_to_all(
        state.reshape(slices, group, row_count, col_count), "tm", 0, 0, tiled=True
    ).reshape(slices * group, row_count, col_count)
    my_params = lax.dynamic_slice_in_dim(params, slice_index * group, group, 0)
    spread_params = jnp.repeat(my_params, band_width, axis=1)

    fields = jnp.stack([diffusivity, velocity_x, velocity_y, source_shape])
    own = jnp.concatenate([mine, fields])
    wide_fields = with_halo(fields, "space", depth)
    wide = jnp.concatenate([with_halo(mine, "space", depth), wide_fields])
    count = slices * group
    global_rows = first_row - depth + jnp.arange(row_count + 2 * depth, dtype=jnp.int32)
    wide_inside = ((global_rows >= 0) & (global_rows < slabs)).astype(jnp.float32)[:, None]

    def block_steps(block, inside):
        states = block[:count]
        coeffs = block[count : count + 3]
        forcing = jnp.tile(block[count + 3][None] * spread_params[:, None, :], (slices, 1, 1))

        def step(values, off, step_size, q):
            lo, hi = off + 1, off + values.shape[1] - 1
            q = None if q is None else q[:, lo:hi]
            return advance(values, coeffs[:, lo:hi], inside[lo:hi], step_size, q)

        coarse = step(states, 0, coarse_dt, None)
        current = states
        for section in range(FINE):
            current = step(current, section, FINE_DT, forcing)
        coarse = coarse[:, FINE - 1 : FINE - 1 + current.shape[1]] * later[:, None, None]
        return current - coarse

    later = (jnp.arange(count) >= group).astype(jnp.float32)
    inner = block_steps(own, wide_inside[depth : depth + row_count])
    strip = depth + 2 * FINE
    strips = jnp.concatenate([wide[:, :strip], wide[:, -strip:]], axis=1)
    strips_inside = jnp.concatenate([wide_inside[:strip], wide_inside[-strip:]])
    edges = block_steps(strips, strips_inside)

    def stitch(edges, inner):
        return jnp.concatenate([edges[:, :depth], inner, edges[:, strip : strip + depth]], axis=1)

    current = stitch(edges, inner)
    wide_coeffs = wide[count : count + 3]

    def step(values, low, step_size, forcing):
        n = values.shape[1]
        lo, hi = low + 1, low + n - 1
        q = None if forcing is None else forcing[:, lo:hi]
        return advance(values, wide_coeffs[:, lo:hi], wide_inside[lo:hi], step_size, q)

    fine = current.reshape(slices, group, -1, col_count)
    running = fine[0]
    results = [running[:, links : links + row_count]]
    for link in range(1, slices):
        correction = fine[link]
        stepped = step(running, FINE + link - 1, coarse_dt, None)
        running = correction[:, link : correction.shape[1] - link] + stepped
        results.append(running[:, links - link : links - link + row_count])
    done = jnp.stack(results)
    running = lax.all_to_all(done, "tm", 0, 0, tiled=True).reshape(
        members_here, row_count, col_count
    )
    new_states = running[None]

    local_cell = obs_cell[0] - first_row * col_count
    rows = local_cell // col_count
    cols = local_cell % col_count
    row_pick = (rows[:, None] == jnp.arange(row_count, dtype=jnp.int32)[None, :]).astype(jnp.float32)
    picked_rows = jnp.einsum("or,mrc->moc", row_pick, running, precision=lax.Precision.HIGHEST)
    at_col = lax.broadcasted_iota(jnp.int32, picked_rows.shape, 2) == cols[None, :, None]
    predicted = jnp.sum(jnp.where(at_col, picked_rows, 0.0), axis=2)
    every_pred = both_halves(predicted, "ens")
    every_param = both_halves(params, "ens")
    total = every_pred.shape[0]
    norm_factor = 1.0 / math.sqrt(total - 1)
    inv_spread = lax.rsqrt(obs_var[0])[None, :]
    pred_mean = jnp.mean(every_pred, axis=0, keepdims=True)
    anomaly = (every_pred - pred_mean) * (inv_spread * norm_factor)
    misfit = (obs_data[0][None, :] + obs_noise[0].T - every_pred) * inv_spread
    gram = jnp.dot(anomaly, anomaly.T, precision=lax.Precision.HIGHEST)
    cross = jnp.dot(anomaly, misfit.T, precision=lax.Precision.HIGHEST)
    sums = jnp.stack([gram, cross])
    sums = quad_sum(sums, "tm")
    sums = quad_sum(sums, "space")
    gram, cross = sums[0], sums[1]
    system = jnp.eye(total, dtype=jnp.float32) + gram
    factor = jnp.linalg.cholesky(system)
    weights = jax.scipy.linalg.cho_solve((factor, True), cross)
    param_anom = every_param - jnp.mean(every_param, axis=0)
    own_weights = lax.dynamic_slice_in_dim(
        weights, lax.axis_index("ens") * members_here, members_here, 1
    )
    new_params = (
        params + jnp.dot(own_weights.T, param_anom, precision=lax.Precision.HIGHEST) * norm_factor
    )
    return (new_states, new_params)


def solution(mesh):
    in_specs = (
        P("tm", "ens", "space", None),
        P("space", None),
        P("space", None),
        P("space", None),
        P("space", None),
        P("ens", None),
        P("tm", "space"),
        P("tm", "space"),
        P("tm", "space", None),
        P("tm", "space"),
    )
    out_specs = (P("tm", "ens", "space", None), P("ens", None))
    return jax.shard_map(
        per_device, mesh=mesh, in_specs=in_specs, out_specs=out_specs, check_vma=False
    )
```

```python
import math

import jax
import jax.numpy as jnp
from jax import lax
from jax.sharding import PartitionSpec as P

FINE = 4


FINE_DT = 0.25


def with_halo(cells, axis, width):
    count = lax.axis_size(axis)
    ends = count - 1
    head = cells[:, :width]
    tail = cells[:, cells.shape[1] - width :]
    return jnp.concatenate(
        [
            lax.ppermute(tail, axis, [(i, i + 1) for i in range(ends)]),
            cells,
            lax.ppermute(head, axis, [(i + 1, i) for i in range(ends)]),
        ],
        axis=1,
    )


def quad_sum(value, axis):
    count = lax.axis_size(axis)
    if count & (count - 1):
        return lax.psum(value, axis)
    bit = 1
    while bit < count:
        if bit * 4 <= count:
            near, far, both = (
                lax.ppermute(value, axis, [(i, i ^ (k * bit)) for i in range(count)])
                for k in (1, 2, 3)
            )
            value = (value + near) + (far + both)
            bit *= 4
        else:
            value = value + lax.ppermute(value, axis, [(i, i ^ bit) for i in range(count)])
            bit *= 2
    return value


def both_halves(value, axis):
    other = lax.ppermute(value, axis, [(0, 1), (1, 0)])
    first = lax.axis_index(axis) == 0
    return jnp.where(first, jnp.concatenate([value, other]), jnp.concatenate([other, value]))


def advance(values_in, coeffs, inside, step_size, forcing):
    middle = values_in[:, 1:-1, :]
    above_row = values_in[:, :-2, :]
    below_row = values_in[:, 2:, :]
    west_cell = jnp.pad(middle[:, :, :-1], ((0, 0), (0, 0), (1, 0)))
    east_cell = jnp.pad(middle[:, :, 1:], ((0, 0), (0, 0), (0, 1)))
    spread_term = coeffs[0] * (above_row + below_row + west_cell + east_cell - 4.0 * middle)
    tendency = (
        spread_term
        - coeffs[1] * (east_cell - west_cell) * 0.5
        - coeffs[2] * (below_row - above_row) * 0.5
    )
    if forcing is not None:
        tendency = tendency + forcing
    return (middle + step_size * tendency) * inside


def per_device(
    start_states,
    velocity_x,
    velocity_y,
    diffusivity,
    source_shape,
    params,
    obs_cell,
    obs_data,
    obs_noise,
    obs_var,
):
    coarse_dt = FINE_DT * FINE
    state = start_states[0]
    members_here, row_count, col_count = state.shape
    slabs = row_count * lax.axis_size("space")
    first_row = lax.axis_index("space") * row_count
    slice_index = lax.axis_index("tm")
    slices = lax.axis_size("tm")
    links = slices - 1
    depth = FINE + links
    group = members_here // slices
    band_width = col_count // params.shape[1]

    mine = lax.all_to_all(
        state.reshape(slices, group, row_count, col_count), "tm", 0, 0, tiled=True
    ).reshape(slices * group, row_count, col_count)
    my_params = lax.dynamic_slice_in_dim(params, slice_index * group, group, 0)
    spread_params = jnp.repeat(my_params, band_width, axis=1)

    fields = jnp.stack([diffusivity, velocity_x, velocity_y, source_shape])
    own = jnp.concatenate([mine, fields])
    wide_fields = with_halo(fields, "space", depth)
    wide = jnp.concatenate([with_halo(mine, "space", depth), wide_fields])
    count = slices * group
    global_rows = first_row - depth + jnp.arange(row_count + 2 * depth, dtype=jnp.int32)
    wide_inside = ((global_rows >= 0) & (global_rows < slabs)).astype(jnp.float32)[:, None]

    def block_steps(block, inside):
        states = block[:count]
        coeffs = block[count : count + 3]
        forcing = jnp.tile(block[count + 3][None] * spread_params[:, None, :], (slices, 1, 1))

        def step(values, off, step_size, q):
            lo, hi = off + 1, off + values.shape[1] - 1
            q = None if q is None else q[:, lo:hi]
            return advance(values, coeffs[:, lo:hi], inside[lo:hi], step_size, q)

        coarse = step(states, 0, coarse_dt, None)
        current = states
        for section in range(FINE):
            current = step(current, section, FINE_DT, forcing)
        coarse = coarse[:, FINE - 1 : FINE - 1 + current.shape[1]] * later[:, None, None]
        return current - coarse

    later = (jnp.arange(count) >= group).astype(jnp.float32)
    inner = block_steps(own, wide_inside[depth : depth + row_count])
    strip = depth + 2 * FINE
    strips = jnp.concatenate([wide[:, :strip], wide[:, -strip:]], axis=1)
    strips_inside = jnp.concatenate([wide_inside[:strip], wide_inside[-strip:]])
    edges = block_steps(strips, strips_inside)

    def stitch(edges, inner):
        return jnp.concatenate([edges[:, :depth], inner, edges[:, strip : strip + depth]], axis=1)

    current = stitch(edges, inner)
    wide_coeffs = wide[count : count + 3]

    def step(values, low, step_size, forcing):
        n = values.shape[1]
        lo, hi = low + 1, low + n - 1
        q = None if forcing is None else forcing[:, lo:hi]
        return advance(values, wide_coeffs[:, lo:hi], wide_inside[lo:hi], step_size, q)

    fine = current.reshape(slices, group, -1, col_count)
    running = fine[0]
    results = [running[:, links : links + row_count]]
    for link in range(1, slices):
        correction = fine[link]
        stepped = step(running, FINE + link - 1, coarse_dt, None)
        running = correction[:, link : correction.shape[1] - link] + stepped
        results.append(running[:, links - link : links - link + row_count])
    done = jnp.stack(results)
    running = lax.all_to_all(done, "tm", 0, 0, tiled=True).reshape(
        members_here, row_count, col_count
    )
    new_states = running[None]

    local_cell = obs_cell[0] - first_row * col_count
    rows = local_cell // col_count
    cols = local_cell % col_count
    col_pick = (cols[:, None] == jnp.arange(col_count, dtype=jnp.int32)[None, :]).astype(jnp.float32)
    picked_cols = jnp.einsum("mrc,oc->mro", running, col_pick, precision=lax.Precision.HIGHEST)
    at_row = lax.broadcasted_iota(jnp.int32, picked_cols.shape, 1) == rows[None, None, :]
    predicted = jnp.sum(jnp.where(at_row, picked_cols, 0.0), axis=1)
    every_pred = both_halves(predicted, "ens")
    every_param = both_halves(params, "ens")
    total = every_pred.shape[0]
    norm_factor = 1.0 / math.sqrt(total - 1)
    inv_spread = lax.rsqrt(obs_var[0])[None, :]
    pred_mean = jnp.mean(every_pred, axis=0, keepdims=True)
    anomaly = (every_pred - pred_mean) * (inv_spread * norm_factor)
    misfit = (obs_data[0][None, :] + obs_noise[0].T - every_pred) * inv_spread
    gram = jnp.dot(anomaly, anomaly.T, precision=lax.Precision.HIGHEST)
    cross = jnp.dot(anomaly, misfit.T, precision=lax.Precision.HIGHEST)
    sums = jnp.stack([gram, cross])
    sums = quad_sum(sums, "tm")
    sums = quad_sum(sums, "space")
    gram, cross = sums[0], sums[1]
    system = jnp.eye(total, dtype=jnp.float32) + gram
    factor = jnp.linalg.cholesky(system)
    weights = jax.scipy.linalg.cho_solve((factor, True), cross)
    param_anom = every_param - jnp.mean(every_param, axis=0)
    own_weights = lax.dynamic_slice_in_dim(
        weights, lax.axis_index("ens") * members_here, members_here, 1
    )
    new_params = (
        params + jnp.dot(own_weights.T, param_anom, precision=lax.Precision.HIGHEST) * norm_factor
    )
    return (new_states, new_params)


def solution(mesh):
    in_specs = (
        P("tm", "ens", "space", None),
        P("space", None),
        P("space", None),
        P("space", None),
        P("space", None),
        P("ens", None),
        P("tm", "space"),
        P("tm", "space"),
        P("tm", "space", None),
        P("tm", "space"),
    )
    out_specs = (P("tm", "ens", "space", None), P("ens", None))
    return jax.shard_map(
        per_device, mesh=mesh, in_specs=in_specs, out_specs=out_specs, check_vma=False
    )
```

```python
import math

import jax
import jax.numpy as jnp
from jax import lax
from jax.sharding import PartitionSpec as P

FINE = 4


FINE_DT = 0.25


def with_halo(cells, axis, width):
    count = lax.axis_size(axis)
    ends = count - 1
    head = cells[:, :width]
    tail = cells[:, cells.shape[1] - width :]
    return jnp.concatenate(
        [
            lax.ppermute(tail, axis, [(i, i + 1) for i in range(ends)]),
            cells,
            lax.ppermute(head, axis, [(i + 1, i) for i in range(ends)]),
        ],
        axis=1,
    )


def quad_sum(value, axis):
    count = lax.axis_size(axis)
    if count & (count - 1):
        return lax.psum(value, axis)
    bit = 1
    while bit < count:
        if bit * 4 <= count:
            near, far, both = (
                lax.ppermute(value, axis, [(i, i ^ (k * bit)) for i in range(count)])
                for k in (1, 2, 3)
            )
            value = (value + near) + (far + both)
            bit *= 4
        else:
            value = value + lax.ppermute(value, axis, [(i, i ^ bit) for i in range(count)])
            bit *= 2
    return value


def both_halves(value, axis):
    other = lax.ppermute(value, axis, [(0, 1), (1, 0)])
    first = lax.axis_index(axis) == 0
    return jnp.where(first, jnp.concatenate([value, other]), jnp.concatenate([other, value]))


def advance(values_in, coeffs, inside, step_size, forcing):
    middle = values_in[:, 1:-1, :]
    above_row = values_in[:, :-2, :]
    below_row = values_in[:, 2:, :]
    west_cell = jnp.pad(middle[:, :, :-1], ((0, 0), (0, 0), (1, 0)))
    east_cell = jnp.pad(middle[:, :, 1:], ((0, 0), (0, 0), (0, 1)))
    spread_term = coeffs[0] * (above_row + below_row + west_cell + east_cell - 4.0 * middle)
    tendency = (
        spread_term
        - coeffs[1] * (east_cell - west_cell) * 0.5
        - coeffs[2] * (below_row - above_row) * 0.5
    )
    if forcing is not None:
        tendency = tendency + forcing
    return (middle + step_size * tendency) * inside


def per_device(
    start_states,
    velocity_x,
    velocity_y,
    diffusivity,
    source_shape,
    params,
    obs_cell,
    obs_data,
    obs_noise,
    obs_var,
):
    coarse_dt = FINE_DT * FINE
    state = start_states[0]
    members_here, row_count, col_count = state.shape
    slabs = row_count * lax.axis_size("space")
    first_row = lax.axis_index("space") * row_count
    slice_index = lax.axis_index("tm")
    slices = lax.axis_size("tm")
    links = slices - 1
    depth = FINE + links
    group = members_here // slices
    band_width = col_count // params.shape[1]

    mine = lax.all_to_all(
        state.reshape(slices, group, row_count, col_count), "tm", 0, 0, tiled=True
    ).reshape(slices * group, row_count, col_count)
    my_params = lax.dynamic_slice_in_dim(params, slice_index * group, group, 0)
    spread_params = jnp.repeat(my_params, band_width, axis=1)

    fields = jnp.stack([diffusivity, velocity_x, velocity_y, source_shape])
    wide_fields = with_halo(fields, "space", depth)
    wide_states = with_halo(mine, "space", depth)
    count = slices * group
    global_rows = first_row - depth + jnp.arange(row_count + 2 * depth, dtype=jnp.int32)
    wide_inside = ((global_rows >= 0) & (global_rows < slabs)).astype(jnp.float32)[:, None]

    def block_steps(states, block, inside):
        coeffs = block[:3]
        forcing = jnp.tile(block[3][None] * spread_params[:, None, :], (slices, 1, 1))

        def step(values, off, step_size, q):
            lo, hi = off + 1, off + values.shape[1] - 1
            q = None if q is None else q[:, lo:hi]
            return advance(values, coeffs[:, lo:hi], inside[lo:hi], step_size, q)

        coarse = step(states, 0, coarse_dt, None)
        current = states
        for section in range(FINE):
            current = step(current, section, FINE_DT, forcing)
        coarse = coarse[:, FINE - 1 : FINE - 1 + current.shape[1]] * later[:, None, None]
        return current - coarse

    later = (jnp.arange(count) >= group).astype(jnp.float32)
    inner = block_steps(mine, fields, wide_inside[depth : depth + row_count])
    strip = depth + 2 * FINE
    strip_states = jnp.concatenate([wide_states[:, :strip], wide_states[:, -strip:]], axis=1)
    strip_fields = jnp.concatenate([wide_fields[:, :strip], wide_fields[:, -strip:]], axis=1)
    strips_inside = jnp.concatenate([wide_inside[:strip], wide_inside[-strip:]])
    edges = block_steps(strip_states, strip_fields, strips_inside)

    def stitch(edges, inner):
        return jnp.concatenate([edges[:, :depth], inner, edges[:, strip : strip + depth]], axis=1)

    current = stitch(edges, inner)
    wide_coeffs = wide_fields[:3]

    def step(values, low, step_size, forcing):
        n = values.shape[1]
        lo, hi = low + 1, low + n - 1
        q = None if forcing is None else forcing[:, lo:hi]
        return advance(values, wide_coeffs[:, lo:hi], wide_inside[lo:hi], step_size, q)

    fine = current.reshape(slices, group, -1, col_count)
    running = fine[0]
    results = [running[:, links : links + row_count]]
    for link in range(1, slices):
        correction = fine[link]
        stepped = step(running, FINE + link - 1, coarse_dt, None)
        running = correction[:, link : correction.shape[1] - link] + stepped
        results.append(running[:, links - link : links - link + row_count])
    done = jnp.stack(results)
    running = lax.all_to_all(done, "tm", 0, 0, tiled=True).reshape(
        members_here, row_count, col_count
    )
    new_states = running[None]

    local_cell = obs_cell[0] - first_row * col_count
    rows = local_cell // col_count
    cols = local_cell % col_count
    col_pick = (cols[:, None] == jnp.arange(col_count, dtype=jnp.int32)[None, :]).astype(jnp.float32)
    picked_cols = jnp.einsum("mrc,oc->mro", running, col_pick, precision=lax.Precision.HIGHEST)
    at_row = lax.broadcasted_iota(jnp.int32, picked_cols.shape, 1) == rows[None, None, :]
    predicted = jnp.sum(jnp.where(at_row, picked_cols, 0.0), axis=1)
    every_pred = both_halves(predicted, "ens")
    every_param = both_halves(params, "ens")
    total = every_pred.shape[0]
    norm_factor = 1.0 / math.sqrt(total - 1)
    inv_spread = lax.rsqrt(obs_var[0])[None, :]
    pred_mean = jnp.mean(every_pred, axis=0, keepdims=True)
    anomaly = (every_pred - pred_mean) * (inv_spread * norm_factor)
    misfit = (obs_data[0][None, :] + obs_noise[0].T - every_pred) * inv_spread
    gram = jnp.dot(anomaly, anomaly.T, precision=lax.Precision.HIGHEST)
    cross = jnp.dot(anomaly, misfit.T, precision=lax.Precision.HIGHEST)
    sums = jnp.stack([gram, cross])
    sums = quad_sum(sums, "tm")
    sums = quad_sum(sums, "space")
    gram, cross = sums[0], sums[1]
    system = jnp.eye(total, dtype=jnp.float32) + gram
    factor = jnp.linalg.cholesky(system)
    weights = jax.scipy.linalg.cho_solve((factor, True), cross)
    param_anom = every_param - jnp.mean(every_param, axis=0)
    own_weights = lax.dynamic_slice_in_dim(
        weights, lax.axis_index("ens") * members_here, members_here, 1
    )
    new_params = (
        params + jnp.dot(own_weights.T, param_anom, precision=lax.Precision.HIGHEST) * norm_factor
    )
    return (new_states, new_params)


def solution(mesh):
    in_specs = (
        P("tm", "ens", "space", None),
        P("space", None),
        P("space", None),
        P("space", None),
        P("space", None),
        P("ens", None),
        P("tm", "space"),
        P("tm", "space"),
        P("tm", "space", None),
        P("tm", "space"),
    )
    out_specs = (P("tm", "ens", "space", None), P("ens", None))
    return jax.shard_map(
        per_device, mesh=mesh, in_specs=in_specs, out_specs=out_specs, check_vma=False
    )
```

```python
import math

import jax
import jax.numpy as jnp
from jax import lax
from jax.sharding import PartitionSpec as P

FINE = 4


FINE_DT = 0.25


def with_halo(cells, axis, width):
    count = lax.axis_size(axis)
    ends = count - 1
    head = cells[:, :width]
    tail = cells[:, cells.shape[1] - width :]
    return jnp.concatenate(
        [
            lax.ppermute(tail, axis, [(i, i + 1) for i in range(ends)]),
            cells,
            lax.ppermute(head, axis, [(i + 1, i) for i in range(ends)]),
        ],
        axis=1,
    )


def quad_sum(value, axis):
    count = lax.axis_size(axis)
    if count & (count - 1):
        return lax.psum(value, axis)
    bit = 1
    while bit < count:
        if bit * 4 <= count:
            near, far, both = (
                lax.ppermute(value, axis, [(i, i ^ (k * bit)) for i in range(count)])
                for k in (1, 2, 3)
            )
            value = (value + near) + (far + both)
            bit *= 4
        else:
            value = value + lax.ppermute(value, axis, [(i, i ^ bit) for i in range(count)])
            bit *= 2
    return value


def both_halves(value, axis):
    other = lax.ppermute(value, axis, [(0, 1), (1, 0)])
    first = lax.axis_index(axis) == 0
    return jnp.where(first, jnp.concatenate([value, other]), jnp.concatenate([other, value]))


def advance(values_in, coeffs, inside, step_size, forcing):
    middle = values_in[:, 1:-1, :]
    above_row = values_in[:, :-2, :]
    below_row = values_in[:, 2:, :]
    west_cell = jnp.pad(middle[:, :, :-1], ((0, 0), (0, 0), (1, 0)))
    east_cell = jnp.pad(middle[:, :, 1:], ((0, 0), (0, 0), (0, 1)))
    spread_term = coeffs[0] * (above_row + below_row + west_cell + east_cell - 4.0 * middle)
    tendency = (
        spread_term
        - coeffs[1] * (east_cell - west_cell) * 0.5
        - coeffs[2] * (below_row - above_row) * 0.5
    )
    if forcing is not None:
        tendency = tendency + forcing
    return (middle + step_size * tendency) * inside


def per_device(
    start_states,
    velocity_x,
    velocity_y,
    diffusivity,
    source_shape,
    params,
    obs_cell,
    obs_data,
    obs_noise,
    obs_var,
):
    coarse_dt = FINE_DT * FINE
    state = start_states[0]
    members_here, row_count, col_count = state.shape
    slabs = row_count * lax.axis_size("space")
    first_row = lax.axis_index("space") * row_count
    slice_index = lax.axis_index("tm")
    slices = lax.axis_size("tm")
    links = slices - 1
    depth = FINE + links
    group = members_here // slices
    band_width = col_count // params.shape[1]

    mine = lax.all_to_all(
        state.reshape(slices, group, row_count, col_count), "tm", 0, 0, tiled=True
    ).reshape(slices * group, row_count, col_count)
    my_params = lax.dynamic_slice_in_dim(params, slice_index * group, group, 0)
    spread_params = jnp.repeat(my_params, band_width, axis=1)

    fields = jnp.stack([diffusivity, velocity_x, velocity_y, source_shape])
    own = jnp.concatenate([mine, fields])
    wide_fields = with_halo(fields, "space", depth)
    wide = jnp.concatenate([with_halo(mine, "space", depth), wide_fields])
    count = slices * group
    global_rows = first_row - depth + jnp.arange(row_count + 2 * depth, dtype=jnp.int32)
    wide_inside = ((global_rows >= 0) & (global_rows < slabs)).astype(jnp.float32)[:, None]

    def block_steps(block, inside):
        states = block[:count]
        coeffs = block[count : count + 3]
        forcing = jnp.tile(block[count + 3][None] * spread_params[:, None, :], (slices, 1, 1))

        def step(values, off, step_size, q):
            lo, hi = off + 1, off + values.shape[1] - 1
            q = None if q is None else q[:, lo:hi]
            return advance(values, coeffs[:, lo:hi], inside[lo:hi], step_size, q)

        coarse = step(states, 0, coarse_dt, None)
        current = states
        for section in range(FINE):
            current = step(current, section, FINE_DT, forcing)
        coarse = coarse[:, FINE - 1 : FINE - 1 + current.shape[1]] * later[:, None, None]
        return current - coarse

    later = (jnp.arange(count) >= group).astype(jnp.float32)
    inner = block_steps(own, wide_inside[depth : depth + row_count])
    strip = depth + 2 * FINE
    strips = jnp.concatenate([wide[:, :strip], wide[:, -strip:]], axis=1)
    strips_inside = jnp.concatenate([wide_inside[:strip], wide_inside[-strip:]])
    edges = block_steps(strips, strips_inside)

    def stitch(edges, inner):
        return jnp.concatenate([edges[:, :depth], inner, edges[:, strip : strip + depth]], axis=1)

    current = stitch(edges, inner)
    wide_coeffs = wide[count : count + 3]

    def step(values, low, step_size, forcing):
        n = values.shape[1]
        lo, hi = low + 1, low + n - 1
        q = None if forcing is None else forcing[:, lo:hi]
        return advance(values, wide_coeffs[:, lo:hi], wide_inside[lo:hi], step_size, q)

    fine = current.reshape(slices, group, -1, col_count)
    running = fine[0]
    results = [running[:, links : links + row_count]]
    for link in range(1, slices):
        correction = fine[link]
        stepped = step(running, FINE + link - 1, coarse_dt, None)
        running = correction[:, link : correction.shape[1] - link] + stepped
        results.append(running[:, links - link : links - link + row_count])
    done = jnp.stack(results)
    running = lax.all_to_all(done, "tm", 0, 0, tiled=True).reshape(
        members_here, row_count, col_count
    )
    new_states = running[None]

    local_cell = obs_cell[0] - first_row * col_count
    rows = local_cell // col_count
    cols = local_cell % col_count
    col_pick = (cols[:, None] == jnp.arange(col_count, dtype=jnp.int32)[None, :]).astype(jnp.float32)
    picked_cols = jnp.einsum("mrc,oc->mro", running, col_pick, precision=lax.Precision.HIGHEST)
    at_row = lax.broadcasted_iota(jnp.int32, picked_cols.shape, 1) == rows[None, None, :]
    predicted = jnp.sum(jnp.where(at_row, picked_cols, 0.0), axis=1)
    every_pred = both_halves(predicted, "ens")
    every_param = both_halves(params, "ens")
    total = every_pred.shape[0]
    norm_factor = 1.0 / math.sqrt(total - 1)
    inv_spread = lax.rsqrt(obs_var[0])[None, :]
    pred_mean = jnp.mean(every_pred, axis=0, keepdims=True)
    anomaly = (every_pred - pred_mean) * (inv_spread * norm_factor)
    misfit = (obs_data[0][None, :] + obs_noise[0].T - every_pred) * inv_spread
    gram = jnp.dot(anomaly, anomaly.T, precision=lax.Precision.HIGHEST)
    cross = jnp.dot(anomaly, misfit.T, precision=lax.Precision.HIGHEST)
    sums = jnp.stack([gram, cross])
    sums = quad_sum(sums, "tm")
    sums = quad_sum(sums, "space")
    gram, cross = sums[0], sums[1]
    system = jnp.eye(total, dtype=jnp.float32) + gram
    factor = jnp.linalg.cholesky(system)
    own_cross = lax.dynamic_slice_in_dim(
        cross, lax.axis_index("ens") * members_here, members_here, 1
    )
    own_weights = jax.scipy.linalg.cho_solve((factor, True), own_cross)
    param_anom = every_param - jnp.mean(every_param, axis=0)
    new_params = (
        params + jnp.dot(own_weights.T, param_anom, precision=lax.Precision.HIGHEST) * norm_factor
    )
    return (new_states, new_params)


def solution(mesh):
    in_specs = (
        P("tm", "ens", "space", None),
        P("space", None),
        P("space", None),
        P("space", None),
        P("space", None),
        P("ens", None),
        P("tm", "space"),
        P("tm", "space"),
        P("tm", "space", None),
        P("tm", "space"),
    )
    out_specs = (P("tm", "ens", "space", None), P("ens", None))
    return jax.shard_map(
        per_device, mesh=mesh, in_specs=in_specs, out_specs=out_specs, check_vma=False
    )
```
